512 devices in a mesh: seq: 64 (over z, x_hi, core), section: 8 (over y, x_lo).
Axes of the slice: x: 4 (x_hi: 2, x_lo: 2; x = x_hi * 2 + x_lo), y: 4, z: 16, core: 2. Of those that a mesh axis runs over, the one named last changes fastest.
Arguments:
- fwd_input: bfloat16 [8, 16384, 768], P('section', 'seq'), may hold values from -6 to 6
- bwd_input: bfloat16 [8, 16384, 768], P('section', 'seq'), may hold values from -6 to 6
- bwd_cotangent: bfloat16 [8, 16384, 768], P('section', 'seq'), may hold values from -6 to 6
- conv_weight: bfloat16 [8, 2, 3, 768, 384], P('section', None, None, 'seq'), may hold values from -0.125 to 0.125
- proj_weight: bfloat16 [8, 2, 384, 768], P('section', None, 'seq'), may hold values from -0.3125 to 0.3125
Outputs:
- next_input: bfloat16 [8, 16384, 768], P('section', 'seq')
- prev_cotangent: bfloat16 [8, 16384, 768], P('section', 'seq')
The draws below stay inside these ranges and needn't reach their ends.
All inputs are finite; a program needn't handle non-finite values.
Results may differ from the reference program's by a relative error of at most 0.012.
Values may be sent and summed in bfloat16 or wider, within the bound.
No kernel may reach another device: no remote copies, remote signals or barrier semaphores. Data moves between devices by JAX's collectives and lax.ppermute only.
A program may use at most 64 MiB of HBM per device.

```python
import jax
import jax.numpy as jnp
from jax import lax

C = 768
H = 384
BLOCKS = 2
FIRST_DILATION = 128
POS = 16384
SECTIONS = 8


def block_scale(rng, shape, shards, least, high):
    def one(dim, shards_of):
        heights = jax.random.uniform(jax.random.fold_in(jax.random.fold_in(rng, 6), dim), (shards_of,), jnp.float32, least / len(shards), high / len(shards))
        return jnp.repeat(jnp.exp(heights), shape[dim] // shards_of).reshape((-1,) + (1,) * (len(shape) - dim - 1))

    level = one(*shards[0])
    for cut in shards[1:]:
        level = level * one(*cut)
    return level


def scatter_about(stream_key, shape, scale, most, pieces=(), kind=jnp.bfloat16):
    loudness = block_scale(stream_key, shape, pieces, -0.22, 0.18) if pieces else 1.0
    drawn = jax.random.normal(stream_key, shape, jnp.float32) * scale * loudness
    return jnp.minimum(jnp.maximum(drawn, -most), most).astype(kind)


def setup_inputs(seed: int = 0) -> dict:
    seeds = jax.random.split(jax.random.key(seed), 6)
    fwd_input = scatter_about(seeds[0], (SECTIONS, POS, C), 1.0, 6.0, ((0, 8), (1, 64)))
    bwd_input = scatter_about(seeds[1], (SECTIONS, POS, C), 1.0, 6.0, ((0, 8), (1, 64)))
    bwd_cotangent = scatter_about(seeds[2], (SECTIONS, POS, C), 1.0, 6.0, ((0, 8), (1, 64)))
    conv_weight = scatter_about(seeds[3], (SECTIONS, BLOCKS, 3, C, H), (3 * C) ** -0.5, 0.125, ((0, 8), (3, 64)))
    proj_weight = scatter_about(seeds[4], (SECTIONS, BLOCKS, H, C), H ** -0.5, 0.3125, ((0, 8), (2, 64)))
    return {"fwd_input": fwd_input, "bwd_input": bwd_input, "bwd_cotangent": bwd_cotangent, "conv_weight": conv_weight, "proj_weight": proj_weight}


def spread(values, spacing_gap):
    width = values.shape[1]
    zeros = jnp.zeros((spacing_gap, width), values.dtype)
    earlier = jnp.concatenate([zeros, values[:-spacing_gap]], 0)
    later = jnp.concatenate([values[spacing_gap:], zeros], 0)
    return (earlier, later)

def gelu_back(value, cotangent):
    return jax.vjp(jax.nn.gelu, value)[1](cotangent)[0]

def rounded(product):
    return lax.optimization_barrier(product.astype(jnp.bfloat16)).astype(jnp.float32)

def section_forward(present_state, conv_weight, proj_weight):
    stored = []
    for depth_level in range(BLOCKS):
        spacing_gap = FIRST_DILATION * 4 ** depth_level
        activated = jax.nn.gelu(present_state.astype(jnp.float32)).astype(jnp.bfloat16)
        earlier, later = spread(activated, spacing_gap)
        preact = rounded(jnp.dot(earlier, conv_weight[depth_level, 0], preferred_element_type=jnp.float32))
        preact = preact + jnp.dot(activated, conv_weight[depth_level, 1], preferred_element_type=jnp.float32)
        preact = preact + rounded(jnp.dot(later, conv_weight[depth_level, 2], preferred_element_type=jnp.float32))
        hidden = jax.nn.gelu(preact).astype(jnp.bfloat16)
        stored.append((present_state, preact))
        branch = jnp.dot(hidden, proj_weight[depth_level], preferred_element_type=jnp.float32)
        present_state = (present_state.astype(jnp.float32) + branch).astype(jnp.bfloat16)
    return (present_state, stored)

def section_backward(present_state, cotangent, conv_weight, proj_weight):
    unused, stored = section_forward(present_state, conv_weight, proj_weight)
    for depth_level in reversed(range(BLOCKS)):
        spacing_gap = FIRST_DILATION * 4 ** depth_level
        block_in, preact = stored[depth_level]
        d_hidden = jnp.dot(cotangent, proj_weight[depth_level].T, preferred_element_type=jnp.float32)
        d_preact = gelu_back(preact, d_hidden).astype(jnp.bfloat16)
        earlier, later = spread(d_preact, spacing_gap)
        d_act = jnp.dot(later, conv_weight[depth_level, 0].T, preferred_element_type=jnp.float32)
        d_act = d_act + jnp.dot(d_preact, conv_weight[depth_level, 1].T, preferred_element_type=jnp.float32)
        d_act = d_act + jnp.dot(earlier, conv_weight[depth_level, 2].T, preferred_element_type=jnp.float32)
        total = cotangent.astype(jnp.float32) + gelu_back(block_in.astype(jnp.float32), d_act)
        cotangent = total.astype(jnp.bfloat16)
    return cotangent

def reference(fwd_input, bwd_input, bwd_cotangent, conv_weight, proj_weight):
    forward_results = []
    backward_outs = []
    for section_num in range(SECTIONS):
        result, unused = section_forward(fwd_input[section_num], conv_weight[section_num], proj_weight[section_num])
        forward_results.append(result)
        backward_outs.append(section_backward(bwd_input[section_num], bwd_cotangent[section_num], conv_weight[section_num], proj_weight[section_num]))
    next_input = jnp.roll(jnp.stack(forward_results, 0), 1, axis=0)
    prev_cotangent = jnp.roll(jnp.stack(backward_outs, 0), -1, axis=0)
    return (next_input, prev_cotangent)
```

```python
import jax
import jax.numpy as jnp
from jax import lax
from jax.sharding import Mesh, PartitionSpec as P

BLOCKS = 2
FIRST_DILATION = 128
SEQ = ("z", "xh", "core")


def seq_size(axis):
    if isinstance(axis, tuple):
        size = 1
        for name in axis:
            size *= lax.axis_size(name)
        return size
    return lax.axis_size(axis)


def padded(x, sides, width):
    for axis, dim in sides:
        size, length = (seq_size(axis), x.shape[dim])
        up = [(i, (i + 1) % size) for i in range(size - 1)]
        down = [(j, i) for i, j in up]
        last = lax.slice_in_dim(x, length - width, length, axis=dim)
        initial = lax.slice_in_dim(x, 0, width, axis=dim)
        before = lax.ppermute(last, axis, up)
        after = lax.ppermute(initial, axis, down)
        x = jnp.concatenate([before, x, after], axis=dim)
    return x


def from_behind(block, axis, distance):
    devices = range(seq_size(axis))
    route = [(i - distance, i) for i in devices if i - distance in devices]
    return lax.ppermute(block, axis, route)


def from_behind_2(block, axis, distance):
    devices = range(seq_size(axis))
    route = [((i - distance) % len(devices), i) for i in devices]
    return lax.ppermute(block, axis, route)


def gelu_back(value, cotangent):
    return jax.vjp(jax.nn.gelu, value)[1](cotangent)[0]


def rounded(product):
    return lax.optimization_barrier(product.astype(jnp.bfloat16)).astype(jnp.float32)


def reach(values, spacing_gap):
    length = values.shape[1]
    if spacing_gap < length:
        padded_input = padded(values, ((SEQ, 1),), spacing_gap)
        return (padded_input[:, :length], padded_input[:, 2 * spacing_gap :])
    shard_hops = spacing_gap // length
    earlier = from_behind(values, SEQ, shard_hops)
    later = from_behind(values, SEQ, -shard_hops)
    return (earlier, later)


def conv_apply(values, weight):
    return jnp.einsum("krc,ch->krh", values, weight, preferred_element_type=jnp.float32)


def conv_transpose(values, weight):
    return jnp.einsum("krh,ch->krc", values, weight, preferred_element_type=jnp.float32)


def run_forward(present_state, pieces):
    stored = []
    for depth_level in range(BLOCKS):
        conv_part, proj_part = pieces[depth_level]
        spacing_gap = FIRST_DILATION * 4**depth_level
        activated = jax.nn.gelu(present_state.astype(jnp.float32)).astype(jnp.bfloat16)
        middle = conv_apply(activated, conv_part[1])
        earlier, later = reach(activated, spacing_gap)
        preact = (
            rounded(conv_apply(earlier, conv_part[0]))
            + middle
            + rounded(conv_apply(later, conv_part[2]))
        )
        hidden = jax.nn.gelu(preact).astype(jnp.bfloat16)
        stored.append((present_state, preact))
        branch = jnp.einsum("krh,hc->krc", hidden, proj_part, preferred_element_type=jnp.float32)
        present_state = (present_state.astype(jnp.float32) + branch).astype(jnp.bfloat16)
    return (present_state, stored)


def gather_weights(conv_weight, proj_weight):
    flat = jnp.concatenate([conv_weight.reshape(1, -1), proj_weight.reshape(1, -1)], axis=1)
    for axis in reversed(SEQ):
        flat = lax.all_gather(flat, axis, axis=0, tiled=True)
    shards, split = flat.shape[0], conv_weight.size
    conv = flat[:, :split].reshape((shards,) + conv_weight.shape[1:])
    proj = flat[:, split:].reshape((shards,) + proj_weight.shape[1:])
    conv = jnp.moveaxis(conv, 0, 2).reshape(conv_weight.shape[:3] + (-1, conv_weight.shape[4]))
    proj = jnp.moveaxis(proj, 0, 1).reshape(proj_weight.shape[:2] + (-1, proj_weight.shape[3]))
    return conv, proj


def local(fwd_input, bwd_input, bwd_cotangent, conv_weight, proj_weight):
    convolution_complete, proj_full = gather_weights(conv_weight, proj_weight)
    pieces = [
        (convolution_complete[0, depth_level], proj_full[0, depth_level])
        for depth_level in range(BLOCKS)
    ]
    forward_out, unused = run_forward(fwd_input, pieces)
    unused_out, stored = run_forward(bwd_input, pieces)
    cotangent = bwd_cotangent
    for depth_level in reversed(range(BLOCKS)):
        conv_part, proj_part = pieces[depth_level]
        spacing_gap = FIRST_DILATION * 4**depth_level
        block_in, preact = stored[depth_level]
        d_hidden = jnp.einsum(
            "krc,hc->krh", cotangent, proj_part, preferred_element_type=jnp.float32
        )
        d_preact = gelu_back(preact, d_hidden).astype(jnp.bfloat16)
        earlier, later = reach(d_preact, spacing_gap)
        d_act = (
            conv_transpose(later, conv_part[0])
            + conv_transpose(d_preact, conv_part[1])
            + conv_transpose(earlier, conv_part[2])
        )
        total = cotangent.astype(jnp.float32) + gelu_back(block_in.astype(jnp.float32), d_act)
        cotangent = total.astype(jnp.bfloat16)
    next_input = from_behind_2(forward_out, "section", 1)
    prev_cotangent = from_behind_2(cotangent, "section", -1)
    return (next_input, prev_cotangent)


def solution(mesh):
    seq, section = mesh.shape["seq"], mesh.shape["section"]
    split = Mesh(mesh.devices.reshape(seq // 4, 2, 2, section), SEQ + ("section",))
    in_specs = (
        P("section", SEQ, None),
        P("section", SEQ, None),
        P("section", SEQ, None),
        P("section", None, None, SEQ, None),
        P("section", None, SEQ, None),
    )
    out_specs = (P("section", SEQ, None), P("section", SEQ, None))
    return jax.shard_map(local, mesh=split, in_specs=in_specs, out_specs=out_specs, check_vma=False)
```

```python
import jax
import jax.numpy as jnp
from jax import lax
from jax.sharding import Mesh, PartitionSpec as P

BLOCKS = 2
FIRST_DILATION = 128
SEQ = ("z", "xh", "core")


def seq_size(axis):
    if isinstance(axis, tuple):
        size = 1
        for name in axis:
            size *= lax.axis_size(name)
        return size
    return lax.axis_size(axis)


def padded(x, sides, width):
    for axis, dim in sides:
        size, length = (seq_size(axis), x.shape[dim])
        up = [(i, (i + 1) % size) for i in range(size - 1)]
        down = [(j, i) for i, j in up]
        last = lax.slice_in_dim(x, length - width, length, axis=dim)
        initial = lax.slice_in_dim(x, 0, width, axis=dim)
        before = lax.ppermute(last, axis, up)
        after = lax.ppermute(initial, axis, down)
        x = jnp.concatenate([before, x, after], axis=dim)
    return x


def from_behind(block, axis, distance):
    devices = range(seq_size(axis))
    route = [(i - distance, i) for i in devices if i - distance in devices]
    return lax.ppermute(block, axis, route)


def from_behind_2(block, axis, distance):
    devices = range(seq_size(axis))
    route = [((i - distance) % len(devices), i) for i in devices]
    return lax.ppermute(block, axis, route)


def gelu_back(value, cotangent):
    return jax.vjp(jax.nn.gelu, value)[1](cotangent)[0]


def rounded(product):
    return lax.optimization_barrier(product.astype(jnp.bfloat16)).astype(jnp.float32)


def reach(values, spacing_gap):
    length = values.shape[1]
    if spacing_gap < length:
        padded_input = padded(values, ((SEQ, 1),), spacing_gap)
        return (padded_input[:, :length], padded_input[:, 2 * spacing_gap :])
    shard_hops = spacing_gap // length
    earlier = from_behind(values, SEQ, shard_hops)
    later = from_behind(values, SEQ, -shard_hops)
    return (earlier, later)


def conv_apply(values, weight):
    return jnp.einsum("krc,ch->krh", values, weight, preferred_element_type=jnp.float32)


def conv_transpose(values, weight):
    return jnp.einsum("krh,ch->krc", values, weight, preferred_element_type=jnp.float32)


def run_forward(present_state, pieces):
    stored = []
    for depth_level in range(BLOCKS):
        conv_part, proj_part = pieces[depth_level]
        spacing_gap = FIRST_DILATION * 4**depth_level
        activated = jax.nn.gelu(present_state.astype(jnp.float32)).astype(jnp.bfloat16)
        middle = conv_apply(activated, conv_part[1])
        earlier, later = reach(activated, spacing_gap)
        preact = (
            rounded(conv_apply(earlier, conv_part[0]))
            + middle
            + rounded(conv_apply(later, conv_part[2]))
        )
        hidden = jax.nn.gelu(preact).astype(jnp.bfloat16)
        stored.append((present_state, preact))
        branch = jnp.einsum("krh,hc->krc", hidden, proj_part, preferred_element_type=jnp.float32)
        present_state = (present_state.astype(jnp.float32) + branch).astype(jnp.bfloat16)
    return (present_state, stored)


def gather_weights(conv_weight, proj_weight):
    flat = jnp.concatenate([conv_weight.reshape(1, -1), proj_weight.reshape(1, -1)], axis=1)
    for axis in reversed(SEQ):
        flat = lax.all_gather(flat, axis, axis=0, tiled=True)
    shards, split = flat.shape[0], conv_weight.size
    conv = flat[:, :split].reshape((shards,) + conv_weight.shape[1:])
    proj = flat[:, split:].reshape((shards,) + proj_weight.shape[1:])
    conv = jnp.moveaxis(conv, 0, 2).reshape(conv_weight.shape[:3] + (-1, conv_weight.shape[4]))
    proj = jnp.moveaxis(proj, 0, 1).reshape(proj_weight.shape[:2] + (-1, proj_weight.shape[3]))
    return conv, proj


def local(fwd_input, bwd_input, bwd_cotangent, conv_weight, proj_weight):
    convolution_complete, proj_full = gather_weights(conv_weight, proj_weight)
    pieces = [
        (convolution_complete[0, depth_level], proj_full[0, depth_level])
        for depth_level in range(BLOCKS)
    ]
    both_out, both_stored = run_forward(jnp.concatenate([fwd_input, bwd_input], axis=0), pieces)
    forward_out = both_out[:1]
    stored = [(block_in[1:], preact[1:]) for block_in, preact in both_stored]
    cotangent = bwd_cotangent
    for depth_level in reversed(range(BLOCKS)):
        conv_part, proj_part = pieces[depth_level]
        spacing_gap = FIRST_DILATION * 4**depth_level
        block_in, preact = stored[depth_level]
        d_hidden = jnp.einsum(
            "krc,hc->krh", cotangent, proj_part, preferred_element_type=jnp.float32
        )
        d_preact = gelu_back(preact, d_hidden).astype(jnp.bfloat16)
        earlier, later = reach(d_preact, spacing_gap)
        d_act = (
            conv_transpose(later, conv_part[0])
            + conv_transpose(d_preact, conv_part[1])
            + conv_transpose(earlier, conv_part[2])
        )
        total = cotangent.astype(jnp.float32) + gelu_back(block_in.astype(jnp.float32), d_act)
        cotangent = total.astype(jnp.bfloat16)
    next_input = from_behind_2(forward_out, "section", 1)
    prev_cotangent = from_behind_2(cotangent, "section", -1)
    return (next_input, prev_cotangent)


def solution(mesh):
    seq, section = mesh.shape["seq"], mesh.shape["section"]
    split = Mesh(mesh.devices.reshape(seq // 4, 2, 2, section), SEQ + ("section",))
    in_specs = (
        P("section", SEQ, None),
        P("section", SEQ, None),
        P("section", SEQ, None),
        P("section", None, None, SEQ, None),
        P("section", None, SEQ, None),
    )
    out_specs = (P("section", SEQ, None), P("section", SEQ, None))
    return jax.shard_map(local, mesh=split, in_specs=in_specs, out_specs=out_specs, check_vma=False)
```

```python
import jax
import jax.numpy as jnp
from jax import lax
from jax.sharding import Mesh, PartitionSpec as P

BLOCKS = 2
FIRST_DILATION = 128
SEQ = ("z", "xh", "core")


def seq_size(axis):
    if isinstance(axis, tuple):
        size = 1
        for name in axis:
            size *= lax.axis_size(name)
        return size
    return lax.axis_size(axis)


def padded(x, sides, width):
    for axis, dim in sides:
        size, length = (seq_size(axis), x.shape[dim])
        up = [(i, (i + 1) % size) for i in range(size - 1)]
        down = [(j, i) for i, j in up]
        last = lax.slice_in_dim(x, length - width, length, axis=dim)
        initial = lax.slice_in_dim(x, 0, width, axis=dim)
        before = lax.ppermute(last, axis, up)
        after = lax.ppermute(initial, axis, down)
        x = jnp.concatenate([before, x, after], axis=dim)
    return x


def from_behind(block, axis, distance):
    devices = range(seq_size(axis))
    route = [(i - distance, i) for i in devices if i - distance in devices]
    return lax.ppermute(block, axis, route)


def from_behind_2(block, axis, distance):
    devices = range(seq_size(axis))
    route = [((i - distance) % len(devices), i) for i in devices]
    return lax.ppermute(block, axis, route)


def gelu_back(value, cotangent):
    return jax.vjp(jax.nn.gelu, value)[1](cotangent)[0]


def rounded(product):
    return lax.optimization_barrier(product.astype(jnp.bfloat16)).astype(jnp.float32)


def reach(values, spacing_gap):
    length = values.shape[1]
    if spacing_gap < length:
        padded_input = padded(values, ((SEQ, 1),), spacing_gap)
        return (padded_input[:, :length], padded_input[:, 2 * spacing_gap :])
    shard_hops = spacing_gap // length
    earlier = from_behind(values, SEQ, shard_hops)
    later = from_behind(values, SEQ, -shard_hops)
    return (earlier, later)


def conv_apply(values, weight):
    return jnp.einsum("krc,ch->krh", values, weight, preferred_element_type=jnp.float32)


def conv_transpose(values, weight):
    return jnp.einsum("krh,ch->krc", values, weight, preferred_element_type=jnp.float32)


def run_forward(present_state, pieces):
    stored = []
    for depth_level in range(BLOCKS):
        conv_part, proj_part = pieces[depth_level]
        spacing_gap = FIRST_DILATION * 4**depth_level
        activated = jax.nn.gelu(present_state.astype(jnp.float32)).astype(jnp.bfloat16)
        middle = conv_apply(activated, conv_part[1])
        first_tap = conv_apply(activated, conv_part[0]).astype(jnp.bfloat16)
        last_tap = conv_apply(activated, conv_part[2]).astype(jnp.bfloat16)
        earlier, unused_later = reach(first_tap, spacing_gap)
        unused_earlier, later = reach(last_tap, spacing_gap)
        preact = (
            lax.optimization_barrier(earlier).astype(jnp.float32)
            + middle
            + lax.optimization_barrier(later).astype(jnp.float32)
        )
        hidden = jax.nn.gelu(preact).astype(jnp.bfloat16)
        stored.append((present_state, preact))
        branch = jnp.einsum("krh,hc->krc", hidden, proj_part, preferred_element_type=jnp.float32)
        present_state = (present_state.astype(jnp.float32) + branch).astype(jnp.bfloat16)
    return (present_state, stored)


def gather_weights(conv_weight, proj_weight):
    flat = jnp.concatenate([conv_weight.reshape(1, -1), proj_weight.reshape(1, -1)], axis=1)
    for axis in reversed(SEQ):
        flat = lax.all_gather(flat, axis, axis=0, tiled=True)
    shards, split = flat.shape[0], conv_weight.size
    conv = flat[:, :split].reshape((shards,) + conv_weight.shape[1:])
    proj = flat[:, split:].reshape((shards,) + proj_weight.shape[1:])
    conv = jnp.moveaxis(conv, 0, 2).reshape(conv_weight.shape[:3] + (-1, conv_weight.shape[4]))
    proj = jnp.moveaxis(proj, 0, 1).reshape(proj_weight.shape[:2] + (-1, proj_weight.shape[3]))
    return conv, proj


def local(fwd_input, bwd_input, bwd_cotangent, conv_weight, proj_weight):
    convolution_complete, proj_full = gather_weights(conv_weight, proj_weight)
    pieces = [
        (convolution_complete[0, depth_level], proj_full[0, depth_level])
        for depth_level in range(BLOCKS)
    ]
    both_out, both_stored = run_forward(jnp.concatenate([fwd_input, bwd_input], axis=0), pieces)
    forward_out = both_out[:1]
    stored = [(block_in[1:], preact[1:]) for block_in, preact in both_stored]
    cotangent = bwd_cotangent
    for depth_level in reversed(range(BLOCKS)):
        conv_part, proj_part = pieces[depth_level]
        spacing_gap = FIRST_DILATION * 4**depth_level
        block_in, preact = stored[depth_level]
        d_hidden = jnp.einsum(
            "krc,hc->krh", cotangent, proj_part, preferred_element_type=jnp.float32
        )
        d_preact = gelu_back(preact, d_hidden).astype(jnp.bfloat16)
        earlier, later = reach(d_preact, spacing_gap)
        d_act = (
            conv_transpose(later, conv_part[0])
            + conv_transpose(d_preact, conv_part[1])
            + conv_transpose(earlier, conv_part[2])
        )
        total = cotangent.astype(jnp.float32) + gelu_back(block_in.astype(jnp.float32), d_act)
        cotangent = total.astype(jnp.bfloat16)
    next_input = from_behind_2(forward_out, "section", 1)
    prev_cotangent = from_behind_2(cotangent, "section", -1)
    return (next_input, prev_cotangent)


def solution(mesh):
    seq, section = mesh.shape["seq"], mesh.shape["section"]
    split = Mesh(mesh.devices.reshape(seq // 4, 2, 2, section), SEQ + ("section",))
    in_specs = (
        P("section", SEQ, None),
        P("section", SEQ, None),
        P("section", SEQ, None),
        P("section", None, None, SEQ, None),
        P("section", None, SEQ, None),
    )
    out_specs = (P("section", SEQ, None), P("section", SEQ, None))
    return jax.shard_map(local, mesh=split, in_specs=in_specs, out_specs=out_specs, check_vma=False)
```

```python
import jax
import jax.numpy as jnp
from jax import lax
from jax.sharding import Mesh, PartitionSpec as P

BLOCKS = 2
FIRST_DILATION = 128
SEQ = ("z", "xh", "core")


def seq_size(axis):
    if isinstance(axis, tuple):
        size = 1
        for name in axis:
            size *= lax.axis_size(name)
        return size
    return lax.axis_size(axis)


def padded(x, sides, width):
    for axis, dim in sides:
        size, length = (seq_size(axis), x.shape[dim])
        up = [(i, (i + 1) % size) for i in range(size - 1)]
        down = [(j, i) for i, j in up]
        last = lax.slice_in_dim(x, length - width, length, axis=dim)
        initial = lax.slice_in_dim(x, 0, width, axis=dim)
        before = lax.ppermute(last, axis, up)
        after = lax.ppermute(initial, axis, down)
        x = jnp.concatenate([before, x, after], axis=dim)
    return x


def from_behind(block, axis, distance):
    devices = range(seq_size(axis))
    route = [(i - distance, i) for i in devices if i - distance in devices]
    return lax.ppermute(block, axis, route)


def from_behind_2(block, axis, distance):
    devices = range(seq_size(axis))
    route = [((i - distance) % len(devices), i) for i in devices]
    return lax.ppermute(block, axis, route)


def gelu_back(value, cotangent):
    return jax.vjp(jax.nn.gelu, value)[1](cotangent)[0]


def rounded(product):
    return lax.optimization_barrier(product.astype(jnp.bfloat16)).astype(jnp.float32)


def reach(values, spacing_gap):
    length = values.shape[1]
    if spacing_gap < length:
        padded_input = padded(values, ((SEQ, 1),), spacing_gap)
        return (padded_input[:, :length], padded_input[:, 2 * spacing_gap :])
    shard_hops = spacing_gap // length
    earlier = from_behind(values, SEQ, shard_hops)
    later = from_behind(values, SEQ, -shard_hops)
    return (earlier, later)


def conv_apply(values, weight):
    return jnp.einsum("krc,ch->krh", values, weight, preferred_element_type=jnp.float32)


def conv_transpose(values, weight):
    return jnp.einsum("krh,ch->krc", values, weight, preferred_element_type=jnp.float32)


def run_forward(present_state, pieces):
    stored = []
    for depth_level in range(BLOCKS):
        conv_part, proj_part = pieces[depth_level]
        spacing_gap = FIRST_DILATION * 4**depth_level
        activated = jax.nn.gelu(present_state.astype(jnp.float32)).astype(jnp.bfloat16)
        middle = conv_apply(activated, conv_part[1])
        first_tap = conv_apply(activated, conv_part[0]).astype(jnp.bfloat16)
        last_tap = conv_apply(activated, conv_part[2]).astype(jnp.bfloat16)
        earlier, unused_later = reach(first_tap, spacing_gap)
        unused_earlier, later = reach(last_tap, spacing_gap)
        preact = (
            lax.optimization_barrier(earlier).astype(jnp.float32)
            + middle
            + lax.optimization_barrier(later).astype(jnp.float32)
        )
        hidden = jax.nn.gelu(preact).astype(jnp.bfloat16)
        stored.append((present_state, preact))
        branch = jnp.einsum("krh,hc->krc", hidden, proj_part, preferred_element_type=jnp.float32)
        present_state = (present_state.astype(jnp.float32) + branch).astype(jnp.bfloat16)
    return (present_state, stored)


def ring_gather(block):
    rows, width = block.shape
    span, lanes, cores = lax.axis_size("z"), lax.axis_size("xh"), lax.axis_size("core")
    here, core = lax.axis_index("z"), lax.axis_index("core")
    sign = 2 * core - 1
    route = []
    for z in range(span):
        for x in range(lanes):
            route.append(((z * lanes + x) * cores, (((z + 1) % span) * lanes + x) * cores))
            route.append(((z * lanes + x) * cores + 1, (((z - 1) % span) * lanes + x) * cores + 1))
    half = span // 2
    gathered = jnp.zeros((span, rows, width), block.dtype)
    gathered = lax.dynamic_update_slice(gathered, block[None], (here, 0, 0))
    current, received = block, []
    for step in range(1, half + 1):
        current = lax.ppermute(current, SEQ, route)
        received.append(current)
        source = (here + sign * step) % span
        gathered = lax.dynamic_update_slice(gathered, current[None], (source, 0, 0))
    shared = lax.ppermute(jnp.stack(received[: span - half - 1]), "core", [(0, 1), (1, 0)])
    for step in range(1, span - half):
        source = (here - sign * step) % span
        gathered = lax.dynamic_update_slice(gathered, shared[step - 1][None], (source, 0, 0))
    return gathered.reshape(span * rows, width)


def gather_weights(conv_weight, proj_weight):
    flat = jnp.concatenate([conv_weight.reshape(1, -1), proj_weight.reshape(1, -1)], axis=1)
    flat = lax.all_gather(flat, "core", axis=0, tiled=True)
    flat = lax.all_gather(flat, "xh", axis=0, tiled=True)
    flat = ring_gather(flat)
    shards, split = flat.shape[0], conv_weight.size
    conv = flat[:, :split].reshape((shards,) + conv_weight.shape[1:])
    proj = flat[:, split:].reshape((shards,) + proj_weight.shape[1:])
    conv = jnp.moveaxis(conv, 0, 2).reshape(conv_weight.shape[:3] + (-1, conv_weight.shape[4]))
    proj = jnp.moveaxis(proj, 0, 1).reshape(proj_weight.shape[:2] + (-1, proj_weight.shape[3]))
    return conv, proj


def local(fwd_input, bwd_input, bwd_cotangent, conv_weight, proj_weight):
    convolution_complete, proj_full = gather_weights(conv_weight, proj_weight)
    pieces = [
        (convolution_complete[0, depth_level], proj_full[0, depth_level])
        for depth_level in range(BLOCKS)
    ]
    both_out, both_stored = run_forward(jnp.concatenate([fwd_input, bwd_input], axis=0), pieces)
    forward_out = both_out[:1]
    stored = [(block_in[1:], preact[1:]) for block_in, preact in both_stored]
    cotangent = bwd_cotangent
    for depth_level in reversed(range(BLOCKS)):
        conv_part, proj_part = pieces[depth_level]
        spacing_gap = FIRST_DILATION * 4**depth_level
        block_in, preact = stored[depth_level]
        d_hidden = jnp.einsum(
            "krc,hc->krh", cotangent, proj_part, preferred_element_type=jnp.float32
        )
        d_preact = gelu_back(preact, d_hidden).astype(jnp.bfloat16)
        earlier, later = reach(d_preact, spacing_gap)
        d_act = (
            conv_transpose(later, conv_part[0])
            + conv_transpose(d_preact, conv_part[1])
            + conv_transpose(earlier, conv_part[2])
        )
        total = cotangent.astype(jnp.float32) + gelu_back(block_in.astype(jnp.float32), d_act)
        cotangent = total.astype(jnp.bfloat16)
    next_input = from_behind_2(forward_out, "section", 1)
    prev_cotangent = from_behind_2(cotangent, "section", -1)
    return (next_input, prev_cotangent)


def solution(mesh):
    seq, section = mesh.shape["seq"], mesh.shape["section"]
    split = Mesh(mesh.devices.reshape(seq // 4, 2, 2, section), SEQ + ("section",))
    in_specs = (
        P("section", SEQ, None),
        P("section", SEQ, None),
        P("section", SEQ, None),
        P("section", None, None, SEQ, None),
        P("section", None, SEQ, None),
    )
    out_specs = (P("section", SEQ, None), P("section", SEQ, None))
    return jax.shard_map(local, mesh=split, in_specs=in_specs, out_specs=out_specs, check_vma=False)
```

```python
import jax
import jax.numpy as jnp
from jax import lax
from jax.sharding import Mesh, PartitionSpec as P

BLOCKS = 2
FIRST_DILATION = 128
SEQ = ("z", "xh", "core")


def seq_size(axis):
    if isinstance(axis, tuple):
        size = 1
        for name in axis:
            size *= lax.axis_size(name)
        return size
    return lax.axis_size(axis)


def padded(x, sides, width):
    for axis, dim in sides:
        size, length = (seq_size(axis), x.shape[dim])
        up = [(i, (i + 1) % size) for i in range(size - 1)]
        down = [(j, i) for i, j in up]
        last = lax.slice_in_dim(x, length - width, length, axis=dim)
        initial = lax.slice_in_dim(x, 0, width, axis=dim)
        before = lax.ppermute(last, axis, up)
        after = lax.ppermute(initial, axis, down)
        x = jnp.concatenate([before, x, after], axis=dim)
    return x


def from_behind(block, axis, distance):
    devices = range(seq_size(axis))
    route = [(i - distance, i) for i in devices if i - distance in devices]
    return lax.ppermute(block, axis, route)


def from_behind_2(block, axis, distance):
    devices = range(seq_size(axis))
    route = [((i - distance) % len(devices), i) for i in devices]
    return lax.ppermute(block, axis, route)


def gelu_back(value, cotangent):
    return jax.vjp(jax.nn.gelu, value)[1](cotangent)[0]


def rounded(product):
    return lax.optimization_barrier(product.astype(jnp.bfloat16)).astype(jnp.float32)


def reach(values, spacing_gap):
    length = values.shape[1]
    if spacing_gap < length:
        padded_input = padded(values, ((SEQ, 1),), spacing_gap)
        return (padded_input[:, :length], padded_input[:, 2 * spacing_gap :])
    shard_hops = spacing_gap // length
    earlier = from_behind(values, SEQ, shard_hops)
    later = from_behind(values, SEQ, -shard_hops)
    return (earlier, later)


def conv_apply(values, weight):
    return jnp.einsum("krc,ch->krh", values, weight, preferred_element_type=jnp.float32)


def conv_transpose(values, weight):
    return jnp.einsum("krh,ch->krc", values, weight, preferred_element_type=jnp.float32)


def run_forward(present_state, pieces):
    stored = []
    for depth_level in range(BLOCKS):
        conv_part, proj_part = pieces[depth_level]
        spacing_gap = FIRST_DILATION * 4**depth_level
        activated = jax.nn.gelu(present_state.astype(jnp.float32)).astype(jnp.bfloat16)
        middle = conv_apply(activated, conv_part[1])
        first_tap = conv_apply(activated, conv_part[0]).astype(jnp.bfloat16)
        last_tap = conv_apply(activated, conv_part[2]).astype(jnp.bfloat16)
        earlier, unused_later = reach(first_tap, spacing_gap)
        unused_earlier, later = reach(last_tap, spacing_gap)
        preact = (
            lax.optimization_barrier(earlier).astype(jnp.float32)
            + middle
            + lax.optimization_barrier(later).astype(jnp.float32)
        )
        hidden = jax.nn.gelu(preact).astype(jnp.bfloat16)
        stored.append((present_state, preact))
        branch = jnp.einsum("krh,hc->krc", hidden, proj_part, preferred_element_type=jnp.float32)
        present_state = (present_state.astype(jnp.float32) + branch).astype(jnp.bfloat16)
    return (present_state, stored)


def place(conv, proj, block, chip, conv_shape, proj_shape):
    rows, split = block.shape[0], 1
    for size in conv_shape:
        split *= size
    part = block[:, :split].reshape((rows,) + conv_shape[1:])
    part = jnp.moveaxis(part, 0, 2).reshape(conv_shape[:3] + (rows * conv_shape[3], conv_shape[4]))
    conv = lax.dynamic_update_slice(conv, part, (0, 0, 0, chip * rows * conv_shape[3], 0))
    part = block[:, split:].reshape((rows,) + proj_shape[1:])
    part = jnp.moveaxis(part, 0, 1).reshape(proj_shape[:2] + (rows * proj_shape[2], proj_shape[3]))
    proj = lax.dynamic_update_slice(proj, part, (0, 0, chip * rows * proj_shape[2], 0))
    return conv, proj


def gather_weights(conv_weight, proj_weight):
    conv_shape, proj_shape = conv_weight.shape, proj_weight.shape
    block = jnp.concatenate([conv_weight.reshape(1, -1), proj_weight.reshape(1, -1)], axis=1)
    block = lax.all_gather(block, "core", axis=0, tiled=True)
    block = lax.all_gather(block, "xh", axis=0, tiled=True)
    span, lanes, cores = lax.axis_size("z"), lax.axis_size("xh"), lax.axis_size("core")
    here, core = lax.axis_index("z"), lax.axis_index("core")
    sign = 2 * core - 1
    route = []
    for z in range(span):
        for x in range(lanes):
            route.append(((z * lanes + x) * cores, (((z + 1) % span) * lanes + x) * cores))
            route.append(((z * lanes + x) * cores + 1, (((z - 1) % span) * lanes + x) * cores + 1))
    shards = span * lanes * cores
    conv = jnp.zeros(conv_shape[:3] + (shards * conv_shape[3], conv_shape[4]), conv_weight.dtype)
    proj = jnp.zeros(proj_shape[:2] + (shards * proj_shape[2], proj_shape[3]), proj_weight.dtype)
    conv, proj = place(conv, proj, block, here, conv_shape, proj_shape)
    half = span // 2
    current = block
    for step in range(1, half + 1):
        current = lax.ppermute(current, SEQ, route)
        conv, proj = place(conv, proj, current, (here + sign * step) % span, conv_shape, proj_shape)
        if step < span - half:
            peer = lax.ppermute(current, "core", [(0, 1), (1, 0)])
            conv, proj = place(conv, proj, peer, (here - sign * step) % span, conv_shape, proj_shape)
    return conv, proj


def local(fwd_input, bwd_input, bwd_cotangent, conv_weight, proj_weight):
    convolution_complete, proj_full = gather_weights(conv_weight, proj_weight)
    pieces = [
        (convolution_complete[0, depth_level], proj_full[0, depth_level])
        for depth_level in range(BLOCKS)
    ]
    both_out, both_stored = run_forward(jnp.concatenate([fwd_input, bwd_input], axis=0), pieces)
    forward_out = both_out[:1]
    stored = [(block_in[1:], preact[1:]) for block_in, preact in both_stored]
    cotangent = bwd_cotangent
    for depth_level in reversed(range(BLOCKS)):
        conv_part, proj_part = pieces[depth_level]
        spacing_gap = FIRST_DILATION * 4**depth_level
        block_in, preact = stored[depth_level]
        d_hidden = jnp.einsum(
            "krc,hc->krh", cotangent, proj_part, preferred_element_type=jnp.float32
        )
        d_preact = gelu_back(preact, d_hidden).astype(jnp.bfloat16)
        earlier, later = reach(d_preact, spacing_gap)
        d_act = (
            conv_transpose(later, conv_part[0])
            + conv_transpose(d_preact, conv_part[1])
            + conv_transpose(earlier, conv_part[2])
        )
        total = cotangent.astype(jnp.float32) + gelu_back(block_in.astype(jnp.float32), d_act)
        cotangent = total.astype(jnp.bfloat16)
    next_input = from_behind_2(forward_out, "section", 1)
    prev_cotangent = from_behind_2(cotangent, "section", -1)
    return (next_input, prev_cotangent)


def solution(mesh):
    seq, section = mesh.shape["seq"], mesh.shape["section"]
    split = Mesh(mesh.devices.reshape(seq // 4, 2, 2, section), SEQ + ("section",))
    in_specs = (
        P("section", SEQ, None),
        P("section", SEQ, None),
        P("section", SEQ, None),
        P("section", None, None, SEQ, None),
        P("section", None, SEQ, None),
    )
    out_specs = (P("section", SEQ, None), P("section", SEQ, None))
    return jax.shard_map(local, mesh=split, in_specs=in_specs, out_specs=out_specs, check_vma=False)
```

```python
import jax
import jax.numpy as jnp
from jax import lax
from jax.sharding import Mesh, PartitionSpec as P

BLOCKS = 2
FIRST_DILATION = 128
SEQ = ("z", "xh", "core")


def seq_size(axis):
    if isinstance(axis, tuple):
        size = 1
        for name in axis:
            size *= lax.axis_size(name)
        return size
    return lax.axis_size(axis)


def padded(x, sides, width):
    for axis, dim in sides:
        size, length = (seq_size(axis), x.shape[dim])
        up = [(i, (i + 1) % size) for i in range(size - 1)]
        down = [(j, i) for i, j in up]
        last = lax.slice_in_dim(x, length - width, length, axis=dim)
        initial = lax.slice_in_dim(x, 0, width, axis=dim)
        before = lax.ppermute(last, axis, up)
        after = lax.ppermute(initial, axis, down)
        x = jnp.concatenate([before, x, after], axis=dim)
    return x


def from_behind(block, axis, distance):
    devices = range(seq_size(axis))
    route = [(i - distance, i) for i in devices if i - distance in devices]
    return lax.ppermute(block, axis, route)


def from_behind_2(block, axis, distance):
    devices = range(seq_size(axis))
    route = [((i - distance) % len(devices), i) for i in devices]
    return lax.ppermute(block, axis, route)


def gelu_back(value, cotangent):
    return jax.vjp(jax.nn.gelu, value)[1](cotangent)[0]


def rounded(product):
    return lax.optimization_barrier(product.astype(jnp.bfloat16)).astype(jnp.float32)


def reach(values, spacing_gap):
    length = values.shape[1]
    if spacing_gap < length:
        padded_input = padded(values, ((SEQ, 1),), spacing_gap)
        return (padded_input[:, :length], padded_input[:, 2 * spacing_gap :])
    shard_hops = spacing_gap // length
    earlier = from_behind(values, SEQ, shard_hops)
    later = from_behind(values, SEQ, -shard_hops)
    return (earlier, later)


def conv_apply(values, weight):
    return jnp.einsum("krc,ch->krh", values, weight, preferred_element_type=jnp.float32)


def conv_transpose(values, weight):
    return jnp.einsum("krh,ch->krc", values, weight, preferred_element_type=jnp.float32)


def run_forward(present_state, pieces):
    stored = []
    for depth_level in range(BLOCKS):
        conv_part, proj_part = pieces[depth_level]
        spacing_gap = FIRST_DILATION * 4**depth_level
        activated = jax.nn.gelu(present_state.astype(jnp.float32)).astype(jnp.bfloat16)
        middle = conv_apply(activated, conv_part[1])
        first_tap = conv_apply(activated, conv_part[0]).astype(jnp.bfloat16)
        last_tap = conv_apply(activated, conv_part[2]).astype(jnp.bfloat16)
        earlier, unused_later = reach(first_tap, spacing_gap)
        unused_earlier, later = reach(last_tap, spacing_gap)
        preact = (
            lax.optimization_barrier(earlier).astype(jnp.float32)
            + middle
            + lax.optimization_barrier(later).astype(jnp.float32)
        )
        hidden = jax.nn.gelu(preact).astype(jnp.bfloat16)
        stored.append((present_state, preact))
        branch = jnp.einsum("krh,hc->krc", hidden, proj_part, preferred_element_type=jnp.float32)
        present_state = (present_state.astype(jnp.float32) + branch).astype(jnp.bfloat16)
    return (present_state, stored)


def ring_gather(block):
    rows, width = block.shape
    span, lanes, cores = lax.axis_size("z"), lax.axis_size("xh"), lax.axis_size("core")
    here, core = lax.axis_index("z"), lax.axis_index("core")
    sign = 2 * core - 1
    route = []
    for z in range(span):
        for x in range(lanes):
            route.append(((z * lanes + x) * cores, (((z + 1) % span) * lanes + x) * cores))
            route.append(((z * lanes + x) * cores + 1, (((z - 1) % span) * lanes + x) * cores + 1))
    half = span // 2
    gathered = jnp.zeros((span, rows, width), block.dtype)
    gathered = lax.dynamic_update_slice(gathered, block[None], (here, 0, 0))
    current, received = block, []
    for step in range(1, half + 1):
        current = lax.ppermute(current, SEQ, route)
        received.append(current)
        source = (here + sign * step) % span
        gathered = lax.dynamic_update_slice(gathered, current[None], (source, 0, 0))
    shared = lax.ppermute(jnp.stack(received[: span - half - 1]), "core", [(0, 1), (1, 0)])
    for step in range(1, span - half):
        source = (here - sign * step) % span
        gathered = lax.dynamic_update_slice(gathered, shared[step - 1][None], (source, 0, 0))
    return gathered


def ring_gather3(block):
    return ring_gather(block)


def gather_weights(conv_weight, proj_weight):
    conv, proj = conv_weight[0], proj_weight[0]
    taps, width = conv.shape[0] * conv.shape[1], conv.shape[3]
    both = jnp.concatenate([conv.reshape((taps,) + conv.shape[2:]), proj.reshape((-1,) + conv.shape[2:])], axis=0)
    both = lax.all_gather(lax.all_gather(both, "core", axis=0), "xh", axis=0)
    conv = both[:, :, :taps].reshape(both.shape[:2] + conv.shape)
    proj = both[:, :, taps:].reshape(both.shape[:2] + proj.shape)
    chip = conv.shape[0] * conv.shape[1]
    conv = jnp.moveaxis(conv.reshape((chip,) + conv.shape[2:]), 0, 2)
    conv = conv.reshape(taps * chip * conv.shape[3], width)
    proj = jnp.moveaxis(proj.reshape((chip,) + proj.shape[2:]), 0, 1)
    proj = proj.reshape(-1, width)
    conv_rows = conv.shape[0]
    gathered = ring_gather3(jnp.concatenate([conv, proj], axis=0))
    span = gathered.shape[0]
    conv = gathered[:, :conv_rows].reshape((span,) + conv_weight.shape[1:3] + (-1, width))
    conv = jnp.moveaxis(conv, 0, 2).reshape(conv_weight.shape[:3] + (-1, width))
    proj = gathered[:, conv_rows:].reshape((span, proj_weight.shape[1], -1, proj_weight.shape[3]))
    proj = jnp.moveaxis(proj, 0, 1).reshape(proj_weight.shape[:2] + (-1, proj_weight.shape[3]))
    return conv, proj


def local(fwd_input, bwd_input, bwd_cotangent, conv_weight, proj_weight):
    convolution_complete, proj_full = gather_weights(conv_weight, proj_weight)
    pieces = [
        (convolution_complete[0, depth_level], proj_full[0, depth_level])
        for depth_level in range(BLOCKS)
    ]
    both_out, both_stored = run_forward(jnp.concatenate([fwd_input, bwd_input], axis=0), pieces)
    forward_out = both_out[:1]
    stored = [(block_in[1:], preact[1:]) for block_in, preact in both_stored]
    cotangent = bwd_cotangent
    for depth_level in reversed(range(BLOCKS)):
        conv_part, proj_part = pieces[depth_level]
        spacing_gap = FIRST_DILATION * 4**depth_level
        block_in, preact = stored[depth_level]
        d_hidden = jnp.einsum(
            "krc,hc->krh", cotangent, proj_part, preferred_element_type=jnp.float32
        )
        d_preact = gelu_back(preact, d_hidden).astype(jnp.bfloat16)
        earlier, later = reach(d_preact, spacing_gap)
        d_act = (
            conv_transpose(later, conv_part[0])
            + conv_transpose(d_preact, conv_part[1])
            + conv_transpose(earlier, conv_part[2])
        )
        total = cotangent.astype(jnp.float32) + gelu_back(block_in.astype(jnp.float32), d_act)
        cotangent = total.astype(jnp.bfloat16)
    next_input = from_behind_2(forward_out, "section", 1)
    prev_cotangent = from_behind_2(cotangent, "section", -1)
    return (next_input, prev_cotangent)


def solution(mesh):
    seq, section = mesh.shape["seq"], mesh.shape["section"]
    split = Mesh(mesh.devices.reshape(seq // 4, 2, 2, section), SEQ + ("section",))
    in_specs = (
        P("section", SEQ, None),
        P("section", SEQ, None),
        P("section", SEQ, None),
        P("section", None, None, SEQ, None),
        P("section", None, SEQ, None),
    )
    out_specs = (P("section", SEQ, None), P("section", SEQ, None))
    return jax.shard_map(local, mesh=split, in_specs=in_specs, out_specs=out_specs, check_vma=False)
```

```python
import jax
import jax.numpy as jnp
from jax import lax
from jax.sharding import Mesh, PartitionSpec as P

BLOCKS = 2
FIRST_DILATION = 128
SEQ = ("z", "xh", "core")


def seq_size(axis):
    if isinstance(axis, tuple):
        size = 1
        for name in axis:
            size *= lax.axis_size(name)
        return size
    return lax.axis_size(axis)


def padded(x, sides, width):
    for axis, dim in sides:
        size, length = (seq_size(axis), x.shape[dim])
        up = [(i, (i + 1) % size) for i in range(size - 1)]
        down = [(j, i) for i, j in up]
        last = lax.slice_in_dim(x, length - width, length, axis=dim)
        initial = lax.slice_in_dim(x, 0, width, axis=dim)
        before = lax.ppermute(last, axis, up)
        after = lax.ppermute(initial, axis, down)
        x = jnp.concatenate([before, x, after], axis=dim)
    return x


def from_behind(block, axis, distance):
    devices = range(seq_size(axis))
    route = [(i - distance, i) for i in devices if i - distance in devices]
    return lax.ppermute(block, axis, route)


def from_behind_2(block, axis, distance):
    devices = range(seq_size(axis))
    route = [((i - distance) % len(devices), i) for i in devices]
    return lax.ppermute(block, axis, route)


def gelu_back(value, cotangent):
    return jax.vjp(jax.nn.gelu, value)[1](cotangent)[0]


def rounded(product):
    return lax.optimization_barrier(product.astype(jnp.bfloat16)).astype(jnp.float32)


def reach(values, spacing_gap):
    length = values.shape[1]
    if spacing_gap < length:
        padded_input = padded(values, ((SEQ, 1),), spacing_gap)
        return (padded_input[:, :length], padded_input[:, 2 * spacing_gap :])
    shard_hops = spacing_gap // length
    earlier = from_behind(values, SEQ, shard_hops)
    later = from_behind(values, SEQ, -shard_hops)
    return (earlier, later)


def conv_apply(values, weight):
    return jnp.einsum("krc,ch->krh", values, weight, preferred_element_type=jnp.float32)


def conv_transpose(values, weight):
    return jnp.einsum("krh,ch->krc", values, weight, preferred_element_type=jnp.float32)


def run_forward(present_state, pieces):
    stored = []
    for depth_level in range(BLOCKS):
        conv_part, proj_part = pieces[depth_level]
        spacing_gap = FIRST_DILATION * 4**depth_level
        activated = jax.nn.gelu(present_state.astype(jnp.float32)).astype(jnp.bfloat16)
        middle = conv_apply(activated, conv_part[1])
        first_tap = conv_apply(activated, conv_part[0]).astype(jnp.bfloat16)
        last_tap = conv_apply(activated, conv_part[2]).astype(jnp.bfloat16)
        earlier, unused_later = reach(first_tap, spacing_gap)
        unused_earlier, later = reach(last_tap, spacing_gap)
        preact = (
            lax.optimization_barrier(earlier).astype(jnp.float32)
            + middle
            + lax.optimization_barrier(later).astype(jnp.float32)
        )
        hidden = jax.nn.gelu(preact).astype(jnp.bfloat16)
        stored.append((present_state, preact))
        branch = jnp.einsum("krh,hc->krc", hidden, proj_part, preferred_element_type=jnp.float32)
        present_state = (present_state.astype(jnp.float32) + branch).astype(jnp.bfloat16)
    return (present_state, stored)


def ring_gather(block):
    rows, width = block.shape
    span, lanes, cores = lax.axis_size("z"), lax.axis_size("xh"), lax.axis_size("core")
    here, core = lax.axis_index("z"), lax.axis_index("core")
    sign = 2 * core - 1
    route = []
    for z in range(span):
        for x in range(lanes):
            route.append(((z * lanes + x) * cores, (((z + 1) % span) * lanes + x) * cores))
            route.append(((z * lanes + x) * cores + 1, (((z - 1) % span) * lanes + x) * cores + 1))
    half = span // 2
    gathered = jnp.zeros((span, rows, width), block.dtype)
    gathered = lax.dynamic_update_slice(gathered, block[None], (here, 0, 0))
    current, received = block, []
    cut = rows // 2
    for step in range(1, half + 1):
        current = jnp.concatenate(
            [lax.ppermute(current[:cut], SEQ, route), lax.ppermute(current[cut:], SEQ, route)], axis=0
        )
        received.append(current)
        source = (here + sign * step) % span
        gathered = lax.dynamic_update_slice(gathered, current[None], (source, 0, 0))
    shared = lax.ppermute(jnp.stack(received[: span - half - 1]), "core", [(0, 1), (1, 0)])
    for step in range(1, span - half):
        source = (here - sign * step) % span
        gathered = lax.dynamic_update_slice(gathered, shared[step - 1][None], (source, 0, 0))
    return gathered


def ring_gather3(block):
    return ring_gather(block)


def gather_weights(conv_weight, proj_weight):
    conv, proj = conv_weight[0], proj_weight[0]
    taps, width = conv.shape[0] * conv.shape[1], conv.shape[3]
    both = jnp.concatenate([conv.reshape((taps,) + conv.shape[2:]), proj.reshape((-1,) + conv.shape[2:])], axis=0)
    both = lax.all_gather(lax.all_gather(both, "core", axis=0), "xh", axis=0)
    conv = both[:, :, :taps].reshape(both.shape[:2] + conv.shape)
    proj = both[:, :, taps:].reshape(both.shape[:2] + proj.shape)
    chip = conv.shape[0] * conv.shape[1]
    conv = jnp.moveaxis(conv.reshape((chip,) + conv.shape[2:]), 0, 2)
    conv = conv.reshape(taps * chip * conv.shape[3], width)
    proj = jnp.moveaxis(proj.reshape((chip,) + proj.shape[2:]), 0, 1)
    proj = proj.reshape(-1, width)
    conv_rows = conv.shape[0]
    gathered = ring_gather3(jnp.concatenate([conv, proj], axis=0))
    span = gathered.shape[0]
    conv = gathered[:, :conv_rows].reshape((span,) + conv_weight.shape[1:3] + (-1, width))
    conv = jnp.moveaxis(conv, 0, 2).reshape(conv_weight.shape[:3] + (-1, width))
    proj = gathered[:, conv_rows:].reshape((span, proj_weight.shape[1], -1, proj_weight.shape[3]))
    proj = jnp.moveaxis(proj, 0, 1).reshape(proj_weight.shape[:2] + (-1, proj_weight.shape[3]))
    return conv, proj


def local(fwd_input, bwd_input, bwd_cotangent, conv_weight, proj_weight):
    convolution_complete, proj_full = gather_weights(conv_weight, proj_weight)
    pieces = [
        (convolution_complete[0, depth_level], proj_full[0, depth_level])
        for depth_level in range(BLOCKS)
    ]
    both_out, both_stored = run_forward(jnp.concatenate([fwd_input, bwd_input], axis=0), pieces)
    forward_out = both_out[:1]
    stored = [(block_in[1:], preact[1:]) for block_in, preact in both_stored]
    cotangent = bwd_cotangent
    for depth_level in reversed(range(BLOCKS)):
        conv_part, proj_part = pieces[depth_level]
        spacing_gap = FIRST_DILATION * 4**depth_level
        block_in, preact = stored[depth_level]
        d_hidden = jnp.einsum(
            "krc,hc->krh", cotangent, proj_part, preferred_element_type=jnp.float32
        )
        d_preact = gelu_back(preact, d_hidden).astype(jnp.bfloat16)
        earlier, later = reach(d_preact, spacing_gap)
        d_act = (
            conv_transpose(later, conv_part[0])
            + conv_transpose(d_preact, conv_part[1])
            + conv_transpose(earlier, conv_part[2])
        )
        total = cotangent.astype(jnp.float32) + gelu_back(block_in.astype(jnp.float32), d_act)
        cotangent = total.astype(jnp.bfloat16)
    next_input = from_behind_2(forward_out, "section", 1)
    prev_cotangent = from_behind_2(cotangent, "section", -1)
    return (next_input, prev_cotangent)


def solution(mesh):
    seq, section = mesh.shape["seq"], mesh.shape["section"]
    split = Mesh(mesh.devices.reshape(seq // 4, 2, 2, section), SEQ + ("section",))
    in_specs = (
        P("section", SEQ, None),
        P("section", SEQ, None),
        P("section", SEQ, None),
        P("section", None, None, SEQ, None),
        P("section", None, SEQ, None),
    )
    out_specs = (P("section", SEQ, None), P("section", SEQ, None))
    return jax.shard_map(local, mesh=split, in_specs=in_specs, out_specs=out_specs, check_vma=False)
```

```python
import jax
import jax.numpy as jnp
from jax import lax
from jax.sharding import Mesh, PartitionSpec as P

BLOCKS = 2
FIRST_DILATION = 128
SEQ = ("z", "xh", "core")


def seq_size(axis):
    if isinstance(axis, tuple):
        size = 1
        for name in axis:
            size *= lax.axis_size(name)
        return size
    return lax.axis_size(axis)


def padded(x, sides, width):
    for axis, dim in sides:
        size, length = (seq_size(axis), x.shape[dim])
        up = [(i, (i + 1) % size) for i in range(size - 1)]
        down = [(j, i) for i, j in up]
        last = lax.slice_in_dim(x, length - width, length, axis=dim)
        initial = lax.slice_in_dim(x, 0, width, axis=dim)
        before = lax.ppermute(last, axis, up)
        after = lax.ppermute(initial, axis, down)
        x = jnp.concatenate([before, x, after], axis=dim)
    return x


def from_behind(block, axis, distance):
    devices = range(seq_size(axis))
    route = [(i - distance, i) for i in devices if i - distance in devices]
    return lax.ppermute(block, axis, route)


def from_behind_2(block, axis, distance):
    devices = range(seq_size(axis))
    route = [((i - distance) % len(devices), i) for i in devices]
    return lax.ppermute(block, axis, route)


def gelu_back(value, cotangent):
    return jax.vjp(jax.nn.gelu, value)[1](cotangent)[0]


def rounded(product):
    return lax.optimization_barrier(product.astype(jnp.bfloat16)).astype(jnp.float32)


def reach(values, spacing_gap):
    length = values.shape[1]
    if spacing_gap < length:
        padded_input = padded(values, ((SEQ, 1),), spacing_gap)
        return (padded_input[:, :length], padded_input[:, 2 * spacing_gap :])
    shard_hops = spacing_gap // length
    earlier = from_behind(values, SEQ, shard_hops)
    later = from_behind(values, SEQ, -shard_hops)
    return (earlier, later)


def conv_apply(values, weight):
    return jnp.einsum("krc,ch->krh", values, weight, preferred_element_type=jnp.float32)


def conv_transpose(values, weight):
    return jnp.einsum("krh,ch->krc", values, weight, preferred_element_type=jnp.float32)


def run_forward(present_state, pieces):
    stored = []
    for depth_level in range(BLOCKS):
        conv_part, proj_part = pieces[depth_level]
        spacing_gap = FIRST_DILATION * 4**depth_level
        activated = jax.nn.gelu(present_state.astype(jnp.float32)).astype(jnp.bfloat16)
        middle = conv_apply(activated, conv_part[1])
        first_tap = conv_apply(activated, conv_part[0]).astype(jnp.bfloat16)
        last_tap = conv_apply(activated, conv_part[2]).astype(jnp.bfloat16)
        earlier, unused_later = reach(first_tap, spacing_gap)
        unused_earlier, later = reach(last_tap, spacing_gap)
        preact = (
            lax.optimization_barrier(earlier).astype(jnp.float32)
            + middle
            + lax.optimization_barrier(later).astype(jnp.float32)
        )
        hidden = jax.nn.gelu(preact).astype(jnp.bfloat16)
        stored.append((present_state, preact))
        branch = jnp.einsum("krh,hc->krc", hidden, proj_part, preferred_element_type=jnp.float32)
        present_state = (present_state.astype(jnp.float32) + branch).astype(jnp.bfloat16)
    return (present_state, stored)


def ring_gather(block):
    rows, width = block.shape
    span, lanes, cores = lax.axis_size("z"), lax.axis_size("xh"), lax.axis_size("core")
    here, core = lax.axis_index("z"), lax.axis_index("core")
    sign = 2 * core - 1
    route = []
    for z in range(span):
        for x in range(lanes):
            route.append(((z * lanes + x) * cores, (((z + 1) % span) * lanes + x) * cores))
            route.append(((z * lanes + x) * cores + 1, (((z - 1) % span) * lanes + x) * cores + 1))
    half = span // 2
    gathered = jnp.zeros((span, rows, width), block.dtype)
    gathered = lax.dynamic_update_slice(gathered, block[None], (here, 0, 0))
    current, received = block, []
    cut = rows // 2
    for step in range(1, half + 1):
        current = jnp.concatenate(
            [lax.ppermute(current[:cut], SEQ, route), lax.ppermute(current[cut:], SEQ, route)], axis=0
        )
        received.append(current)
        source = (here + sign * step) % span
        gathered = lax.dynamic_update_slice(gathered, current[None], (source, 0, 0))
    shared = lax.ppermute(jnp.stack(received[: span - half - 1]), "core", [(0, 1), (1, 0)])
    for step in range(1, span - half):
        source = (here - sign * step) % span
        gathered = lax.dynamic_update_slice(gathered, shared[step - 1][None], (source, 0, 0))
    return gathered


def ring_gather3(block):
    return ring_gather(block)


def swap_gather(value, axis):
    other = lax.ppermute(value, axis, [(0, 1), (1, 0)])
    first = lax.axis_index(axis) == 0
    return jnp.stack([jnp.where(first, value, other), jnp.where(first, other, value)])


def gather_weights(conv_weight, proj_weight):
    conv, proj = conv_weight[0], proj_weight[0]
    taps, width = conv.shape[0] * conv.shape[1], conv.shape[3]
    both = jnp.concatenate([conv.reshape((taps,) + conv.shape[2:]), proj.reshape((-1,) + conv.shape[2:])], axis=0)
    both = swap_gather(swap_gather(both, "core"), "xh")
    conv = both[:, :, :taps].reshape(both.shape[:2] + conv.shape)
    proj = both[:, :, taps:].reshape(both.shape[:2] + proj.shape)
    chip = conv.shape[0] * conv.shape[1]
    conv = jnp.moveaxis(conv.reshape((chip,) + conv.shape[2:]), 0, 2)
    conv = conv.reshape(taps * chip * conv.shape[3], width)
    proj = jnp.moveaxis(proj.reshape((chip,) + proj.shape[2:]), 0, 1)
    proj = proj.reshape(-1, width)
    conv_rows = conv.shape[0]
    gathered = ring_gather3(jnp.concatenate([conv, proj], axis=0))
    span = gathered.shape[0]
    conv = gathered[:, :conv_rows].reshape((span,) + conv_weight.shape[1:3] + (-1, width))
    conv = jnp.moveaxis(conv, 0, 2).reshape(conv_weight.shape[:3] + (-1, width))
    proj = gathered[:, conv_rows:].reshape((span, proj_weight.shape[1], -1, proj_weight.shape[3]))
    proj = jnp.moveaxis(proj, 0, 1).reshape(proj_weight.shape[:2] + (-1, proj_weight.shape[3]))
    return conv, proj


def local(fwd_input, bwd_input, bwd_cotangent, conv_weight, proj_weight):
    convolution_complete, proj_full = gather_weights(conv_weight, proj_weight)
    pieces = [
        (convolution_complete[0, depth_level], proj_full[0, depth_level])
        for depth_level in range(BLOCKS)
    ]
    both_out, both_stored = run_forward(jnp.concatenate([fwd_input, bwd_input], axis=0), pieces)
    forward_out = both_out[:1]
    stored = [(block_in[1:], preact[1:]) for block_in, preact in both_stored]
    cotangent = bwd_cotangent
    for depth_level in reversed(range(BLOCKS)):
        conv_part, proj_part = pieces[depth_level]
        spacing_gap = FIRST_DILATION * 4**depth_level
        block_in, preact = stored[depth_level]
        d_hidden = jnp.einsum(
            "krc,hc->krh", cotangent, proj_part, preferred_element_type=jnp.float32
        )
        d_preact = gelu_back(preact, d_hidden).astype(jnp.bfloat16)
        earlier, later = reach(d_preact, spacing_gap)
        d_act = (
            conv_transpose(later, conv_part[0])
            + conv_transpose(d_preact, conv_part[1])
            + conv_transpose(earlier, conv_part[2])
        )
        total = cotangent.astype(jnp.float32) + gelu_back(block_in.astype(jnp.float32), d_act)
        cotangent = total.astype(jnp.bfloat16)
    next_input = from_behind_2(forward_out, "section", 1)
    prev_cotangent = from_behind_2(cotangent, "section", -1)
    return (next_input, prev_cotangent)


def solution(mesh):
    seq, section = mesh.shape["seq"], mesh.shape["section"]
    split = Mesh(mesh.devices.reshape(seq // 4, 2, 2, section), SEQ + ("section",))
    in_specs = (
        P("section", SEQ, None),
        P("section", SEQ, None),
        P("section", SEQ, None),
        P("section", None, None, SEQ, None),
        P("section", None, SEQ, None),
    )
    out_specs = (P("section", SEQ, None), P("section", SEQ, None))
    return jax.shard_map(local, mesh=split, in_specs=in_specs, out_specs=out_specs, check_vma=False)
```

```python
import jax
import jax.numpy as jnp
from jax import lax
from jax.sharding import Mesh, PartitionSpec as P

BLOCKS = 2
FIRST_DILATION = 128
SEQ = ("z", "xh", "core")


def seq_size(axis):
    if isinstance(axis, tuple):
        size = 1
        for name in axis:
            size *= lax.axis_size(name)
        return size
    return lax.axis_size(axis)


def padded(x, sides, width):
    for axis, dim in sides:
        size, length = (seq_size(axis), x.shape[dim])
        up = [(i, (i + 1) % size) for i in range(size - 1)]
        down = [(j, i) for i, j in up]
        last = lax.slice_in_dim(x, length - width, length, axis=dim)
        initial = lax.slice_in_dim(x, 0, width, axis=dim)
        before = lax.ppermute(last, axis, up)
        after = lax.ppermute(initial, axis, down)
        x = jnp.concatenate([before, x, after], axis=dim)
    return x


def from_behind(block, axis, distance):
    devices = range(seq_size(axis))
    route = [(i - distance, i) for i in devices if i - distance in devices]
    return lax.ppermute(block, axis, route)


def from_behind_2(block, axis, distance):
    devices = range(seq_size(axis))
    route = [((i - distance) % len(devices), i) for i in devices]
    return lax.ppermute(block, axis, route)


def gelu_back(value, cotangent):
    return jax.vjp(jax.nn.gelu, value)[1](cotangent)[0]


def rounded(product):
    return lax.optimization_barrier(product.astype(jnp.bfloat16)).astype(jnp.float32)


def reach(values, spacing_gap):
    length = values.shape[1]
    if spacing_gap < length:
        padded_input = padded(values, ((SEQ, 1),), spacing_gap)
        return (padded_input[:, :length], padded_input[:, 2 * spacing_gap :])
    shard_hops = spacing_gap // length
    earlier = from_behind(values, SEQ, shard_hops)
    later = from_behind(values, SEQ, -shard_hops)
    return (earlier, later)


def conv_apply(values, weight):
    return jnp.einsum("krc,ch->krh", values, weight, preferred_element_type=jnp.float32)


def conv_transpose(values, weight):
    return jnp.einsum("krh,ch->krc", values, weight, preferred_element_type=jnp.float32)


def run_forward(present_state, pieces, first=0):
    stored = []
    for depth_level in range(first, first + len(pieces)):
        conv_part, proj_part = pieces[depth_level - first]
        spacing_gap = FIRST_DILATION * 4**depth_level
        activated = jax.nn.gelu(present_state.astype(jnp.float32)).astype(jnp.bfloat16)
        middle = conv_apply(activated, conv_part[1])
        first_tap = conv_apply(activated, conv_part[0]).astype(jnp.bfloat16)
        last_tap = conv_apply(activated, conv_part[2]).astype(jnp.bfloat16)
        earlier, unused_later = reach(first_tap, spacing_gap)
        unused_earlier, later = reach(last_tap, spacing_gap)
        preact = (
            lax.optimization_barrier(earlier).astype(jnp.float32)
            + middle
            + lax.optimization_barrier(later).astype(jnp.float32)
        )
        hidden = jax.nn.gelu(preact).astype(jnp.bfloat16)
        stored.append((present_state, preact))
        branch = jnp.einsum("krh,hc->krc", hidden, proj_part, preferred_element_type=jnp.float32)
        present_state = (present_state.astype(jnp.float32) + branch).astype(jnp.bfloat16)
    return (present_state, stored)


def ring_gather(block):
    rows, width = block.shape
    span, lanes, cores = lax.axis_size("z"), lax.axis_size("xh"), lax.axis_size("core")
    here, core = lax.axis_index("z"), lax.axis_index("core")
    sign = 2 * core - 1
    route = []
    for z in range(span):
        for x in range(lanes):
            route.append(((z * lanes + x) * cores, (((z + 1) % span) * lanes + x) * cores))
            route.append(((z * lanes + x) * cores + 1, (((z - 1) % span) * lanes + x) * cores + 1))
    half = span // 2
    gathered = jnp.zeros((span, rows, width), block.dtype)
    gathered = lax.dynamic_update_slice(gathered, block[None], (here, 0, 0))
    current, received = block, []
    cut = rows // 2
    for step in range(1, half + 1):
        current = jnp.concatenate(
            [lax.ppermute(current[:cut], SEQ, route), lax.ppermute(current[cut:], SEQ, route)], axis=0
        )
        received.append(current)
        source = (here + sign * step) % span
        gathered = lax.dynamic_update_slice(gathered, current[None], (source, 0, 0))
    shared = lax.ppermute(jnp.stack(received[: span - half - 1]), "core", [(0, 1), (1, 0)])
    for step in range(1, span - half):
        source = (here - sign * step) % span
        gathered = lax.dynamic_update_slice(gathered, shared[step - 1][None], (source, 0, 0))
    return gathered


def ring_gather3(block):
    return ring_gather(block)


def gather_weights(conv_weight, proj_weight):
    conv, proj = conv_weight[0], proj_weight[0]
    taps, width = conv.shape[0] * conv.shape[1], conv.shape[3]
    both = jnp.concatenate([conv.reshape((taps,) + conv.shape[2:]), proj.reshape((-1,) + conv.shape[2:])], axis=0)
    both = lax.all_gather(lax.all_gather(both, "core", axis=0), "xh", axis=0)
    conv = both[:, :, :taps].reshape(both.shape[:2] + conv.shape)
    proj = both[:, :, taps:].reshape(both.shape[:2] + proj.shape)
    chip = conv.shape[0] * conv.shape[1]
    conv = jnp.moveaxis(conv.reshape((chip,) + conv.shape[2:]), 0, 2)
    conv = conv.reshape(taps * chip * conv.shape[3], width)
    proj = jnp.moveaxis(proj.reshape((chip,) + proj.shape[2:]), 0, 1)
    proj = proj.reshape(-1, width)
    conv_rows = conv.shape[0]
    gathered = ring_gather3(jnp.concatenate([conv, proj], axis=0))
    span = gathered.shape[0]
    conv = gathered[:, :conv_rows].reshape((span,) + conv_weight.shape[1:3] + (-1, width))
    conv = jnp.moveaxis(conv, 0, 2).reshape(conv_weight.shape[:3] + (-1, width))
    proj = gathered[:, conv_rows:].reshape((span, proj_weight.shape[1], -1, proj_weight.shape[3]))
    proj = jnp.moveaxis(proj, 0, 1).reshape(proj_weight.shape[:2] + (-1, proj_weight.shape[3]))
    return conv, proj


def local(fwd_input, bwd_input, bwd_cotangent, conv_weight, proj_weight):
    convolution_complete, proj_full = gather_weights(conv_weight, proj_weight)
    pieces = [
        (convolution_complete[0, depth_level], proj_full[0, depth_level])
        for depth_level in range(BLOCKS)
    ]
    both_mid, both_stored = run_forward(jnp.concatenate([fwd_input, bwd_input], axis=0), pieces[:1])
    stored = [(block_in[1:], preact[1:]) for block_in, preact in both_stored]
    unused_out, later_stored = run_forward(both_mid[1:], pieces[1:], first=1)
    stored = stored + later_stored
    forward_out, unused = run_forward(both_mid[:1], pieces[1:], first=1)
    cotangent = bwd_cotangent
    for depth_level in reversed(range(BLOCKS)):
        conv_part, proj_part = pieces[depth_level]
        spacing_gap = FIRST_DILATION * 4**depth_level
        block_in, preact = stored[depth_level]
        d_hidden = jnp.einsum(
            "krc,hc->krh", cotangent, proj_part, preferred_element_type=jnp.float32
        )
        d_preact = gelu_back(preact, d_hidden).astype(jnp.bfloat16)
        earlier, later = reach(d_preact, spacing_gap)
        d_act = (
            conv_transpose(later, conv_part[0])
            + conv_transpose(d_preact, conv_part[1])
            + conv_transpose(earlier, conv_part[2])
        )
        total = cotangent.astype(jnp.float32) + gelu_back(block_in.astype(jnp.float32), d_act)
        cotangent = total.astype(jnp.bfloat16)
    next_input = from_behind_2(forward_out, "section", 1)
    prev_cotangent = from_behind_2(cotangent, "section", -1)
    return (next_input, prev_cotangent)


def solution(mesh):
    seq, section = mesh.shape["seq"], mesh.shape["section"]
    split = Mesh(mesh.devices.reshape(seq // 4, 2, 2, section), SEQ + ("section",))
    in_specs = (
        P("section", SEQ, None),
        P("section", SEQ, None),
        P("section", SEQ, None),
        P("section", None, None, SEQ, None),
        P("section", None, SEQ, None),
    )
    out_specs = (P("section", SEQ, None), P("section", SEQ, None))
    return jax.shard_map(local, mesh=split, in_specs=in_specs, out_specs=out_specs, check_vma=False)
```

```python
import jax
import jax.numpy as jnp
from jax import lax
from jax.sharding import Mesh, PartitionSpec as P

BLOCKS = 2
FIRST_DILATION = 128
SEQ = ("z", "xh", "core")


def seq_size(axis):
    if isinstance(axis, tuple):
        size = 1
        for name in axis:
            size *= lax.axis_size(name)
        return size
    return lax.axis_size(axis)


def padded(x, sides, width):
    for axis, dim in sides:
        size, length = (seq_size(axis), x.shape[dim])
        up = [(i, (i + 1) % size) for i in range(size - 1)]
        down = [(j, i) for i, j in up]
        last = lax.slice_in_dim(x, length - width, length, axis=dim)
        initial = lax.slice_in_dim(x, 0, width, axis=dim)
        before = lax.ppermute(last, axis, up)
        after = lax.ppermute(initial, axis, down)
        x = jnp.concatenate([before, x, after], axis=dim)
    return x


def from_behind(block, axis, distance):
    devices = range(seq_size(axis))
    route = [(i - distance, i) for i in devices if i - distance in devices]
    cut = block.shape[1] // 2
    return jnp.concatenate(
        [lax.ppermute(block[:, :cut], axis, route), lax.ppermute(block[:, cut:], axis, route)], axis=1
    )


def from_behind_2(block, axis, distance):
    devices = range(seq_size(axis))
    route = [((i - distance) % len(devices), i) for i in devices]
    return lax.ppermute(block, axis, route)


def gelu_back(value, cotangent):
    return jax.vjp(jax.nn.gelu, value)[1](cotangent)[0]


def rounded(product):
    return lax.optimization_barrier(product.astype(jnp.bfloat16)).astype(jnp.float32)


def reach(values, spacing_gap):
    length = values.shape[1]
    if spacing_gap < length:
        padded_input = padded(values, ((SEQ, 1),), spacing_gap)
        return (padded_input[:, :length], padded_input[:, 2 * spacing_gap :])
    shard_hops = spacing_gap // length
    earlier = from_behind(values, SEQ, shard_hops)
    later = from_behind(values, SEQ, -shard_hops)
    return (earlier, later)


def conv_apply(values, weight):
    return jnp.einsum("krc,ch->krh", values, weight, preferred_element_type=jnp.float32)


def conv_transpose(values, weight):
    return jnp.einsum("krh,ch->krc", values, weight, preferred_element_type=jnp.float32)


def run_forward(present_state, pieces):
    stored = []
    for depth_level in range(BLOCKS):
        conv_part, proj_part = pieces[depth_level]
        spacing_gap = FIRST_DILATION * 4**depth_level
        activated = jax.nn.gelu(present_state.astype(jnp.float32)).astype(jnp.bfloat16)
        middle = conv_apply(activated, conv_part[1])
        first_tap = conv_apply(activated, conv_part[0]).astype(jnp.bfloat16)
        last_tap = conv_apply(activated, conv_part[2]).astype(jnp.bfloat16)
        earlier, unused_later = reach(first_tap, spacing_gap)
        unused_earlier, later = reach(last_tap, spacing_gap)
        preact = (
            lax.optimization_barrier(earlier).astype(jnp.float32)
            + middle
            + lax.optimization_barrier(later).astype(jnp.float32)
        )
        hidden = jax.nn.gelu(preact).astype(jnp.bfloat16)
        stored.append((present_state, preact))
        branch = jnp.einsum("krh,hc->krc", hidden, proj_part, preferred_element_type=jnp.float32)
        present_state = (present_state.astype(jnp.float32) + branch).astype(jnp.bfloat16)
    return (present_state, stored)


def ring_gather(block):
    rows, width = block.shape
    span, lanes, cores = lax.axis_size("z"), lax.axis_size("xh"), lax.axis_size("core")
    here, core = lax.axis_index("z"), lax.axis_index("core")
    sign = 2 * core - 1
    route = []
    for z in range(span):
        for x in range(lanes):
            route.append(((z * lanes + x) * cores, (((z + 1) % span) * lanes + x) * cores))
            route.append(((z * lanes + x) * cores + 1, (((z - 1) % span) * lanes + x) * cores + 1))
    half = span // 2
    gathered = jnp.zeros((span, rows, width), block.dtype)
    gathered = lax.dynamic_update_slice(gathered, block[None], (here, 0, 0))
    current, received = block, []
    cut = rows // 2
    for step in range(1, half + 1):
        current = jnp.concatenate(
            [lax.ppermute(current[:cut], SEQ, route), lax.ppermute(current[cut:], SEQ, route)], axis=0
        )
        received.append(current)
        source = (here + sign * step) % span
        gathered = lax.dynamic_update_slice(gathered, current[None], (source, 0, 0))
    shared = lax.ppermute(jnp.stack(received[: span - half - 1]), "core", [(0, 1), (1, 0)])
    for step in range(1, span - half):
        source = (here - sign * step) % span
        gathered = lax.dynamic_update_slice(gathered, shared[step - 1][None], (source, 0, 0))
    return gathered


def ring_gather3(block):
    return ring_gather(block)


def gather_weights(conv_weight, proj_weight):
    conv, proj = conv_weight[0], proj_weight[0]
    taps, width = conv.shape[0] * conv.shape[1], conv.shape[3]
    both = jnp.concatenate([conv.reshape((taps,) + conv.shape[2:]), proj.reshape((-1,) + conv.shape[2:])], axis=0)
    both = lax.all_gather(lax.all_gather(both, "core", axis=0), "xh", axis=0)
    conv = both[:, :, :taps].reshape(both.shape[:2] + conv.shape)
    proj = both[:, :, taps:].reshape(both.shape[:2] + proj.shape)
    chip = conv.shape[0] * conv.shape[1]
    conv = jnp.moveaxis(conv.reshape((chip,) + conv.shape[2:]), 0, 2)
    conv = conv.reshape(taps * chip * conv.shape[3], width)
    proj = jnp.moveaxis(proj.reshape((chip,) + proj.shape[2:]), 0, 1)
    proj = proj.reshape(-1, width)
    conv_rows = conv.shape[0]
    gathered = ring_gather3(jnp.concatenate([conv, proj], axis=0))
    span = gathered.shape[0]
    conv = gathered[:, :conv_rows].reshape((span,) + conv_weight.shape[1:3] + (-1, width))
    conv = jnp.moveaxis(conv, 0, 2).reshape(conv_weight.shape[:3] + (-1, width))
    proj = gathered[:, conv_rows:].reshape((span, proj_weight.shape[1], -1, proj_weight.shape[3]))
    proj = jnp.moveaxis(proj, 0, 1).reshape(proj_weight.shape[:2] + (-1, proj_weight.shape[3]))
    return conv, proj


def local(fwd_input, bwd_input, bwd_cotangent, conv_weight, proj_weight):
    convolution_complete, proj_full = gather_weights(conv_weight, proj_weight)
    pieces = [
        (convolution_complete[0, depth_level], proj_full[0, depth_level])
        for depth_level in range(BLOCKS)
    ]
    both_out, both_stored = run_forward(jnp.concatenate([fwd_input, bwd_input], axis=0), pieces)
    forward_out = both_out[:1]
    stored = [(block_in[1:], preact[1:]) for block_in, preact in both_stored]
    cotangent = bwd_cotangent
    for depth_level in reversed(range(BLOCKS)):
        conv_part, proj_part = pieces[depth_level]
        spacing_gap = FIRST_DILATION * 4**depth_level
        block_in, preact = stored[depth_level]
        d_hidden = jnp.einsum(
            "krc,hc->krh", cotangent, proj_part, preferred_element_type=jnp.float32
        )
        d_preact = gelu_back(preact, d_hidden).astype(jnp.bfloat16)
        earlier, later = reach(d_preact, spacing_gap)
        d_act = (
            conv_transpose(later, conv_part[0])
            + conv_transpose(d_preact, conv_part[1])
            + conv_transpose(earlier, conv_part[2])
        )
        total = cotangent.astype(jnp.float32) + gelu_back(block_in.astype(jnp.float32), d_act)
        cotangent = total.astype(jnp.bfloat16)
    next_input = from_behind_2(forward_out, "section", 1)
    prev_cotangent = from_behind_2(cotangent, "section", -1)
    return (next_input, prev_cotangent)


def solution(mesh):
    seq, section = mesh.shape["seq"], mesh.shape["section"]
    split = Mesh(mesh.devices.reshape(seq // 4, 2, 2, section), SEQ + ("section",))
    in_specs = (
        P("section", SEQ, None),
        P("section", SEQ, None),
        P("section", SEQ, None),
        P("section", None, None, SEQ, None),
        P("section", None, SEQ, None),
    )
    out_specs = (P("section", SEQ, None), P("section", SEQ, None))
    return jax.shard_map(local, mesh=split, in_specs=in_specs, out_specs=out_specs, check_vma=False)
```

```python
import jax
import jax.numpy as jnp
from jax import lax
from jax.sharding import Mesh, PartitionSpec as P

BLOCKS = 2
FIRST_DILATION = 128
SEQ = ("z", "xh", "core")


def seq_size(axis):
    if isinstance(axis, tuple):
        size = 1
        for name in axis:
            size *= lax.axis_size(name)
        return size
    return lax.axis_size(axis)


def padded(x, sides, width):
    for axis, dim in sides:
        size, length = (seq_size(axis), x.shape[dim])
        up = [(i, (i + 1) % size) for i in range(size - 1)]
        down = [(j, i) for i, j in up]
        last = lax.slice_in_dim(x, length - width, length, axis=dim)
        initial = lax.slice_in_dim(x, 0, width, axis=dim)
        before = lax.ppermute(last, axis, up)
        after = lax.ppermute(initial, axis, down)
        x = jnp.concatenate([before, x, after], axis=dim)
    return x


def from_behind(block, axis, distance):
    devices = range(seq_size(axis))
    route = [(i - distance, i) for i in devices if i - distance in devices]
    return lax.ppermute(block, axis, route)


def from_behind_2(block, axis, distance):
    devices = range(seq_size(axis))
    route = [((i - distance) % len(devices), i) for i in devices]
    return lax.ppermute(block, axis, route)


def gelu_back(value, cotangent):
    return jax.vjp(jax.nn.gelu, value)[1](cotangent)[0]


def rounded(product):
    return lax.optimization_barrier(product.astype(jnp.bfloat16)).astype(jnp.float32)


def reach(values, spacing_gap):
    length = values.shape[1]
    if spacing_gap < length:
        padded_input = padded(values, ((SEQ, 1),), spacing_gap)
        return (padded_input[:, :length], padded_input[:, 2 * spacing_gap :])
    shard_hops = spacing_gap // length
    earlier = from_behind(values, SEQ, shard_hops)
    later = from_behind(values, SEQ, -shard_hops)
    return (earlier, later)


def conv_apply(values, weight):
    return jnp.einsum("krc,ch->krh", values, weight, preferred_element_type=jnp.float32)


def conv_transpose(values, weight):
    return jnp.einsum("krh,ch->krc", values, weight, preferred_element_type=jnp.float32)


def run_forward(present_state, pieces):
    stored = []
    for depth_level in range(BLOCKS):
        conv_part, proj_part = pieces[depth_level]
        spacing_gap = FIRST_DILATION * 4**depth_level
        activated = jax.nn.gelu(present_state.astype(jnp.float32)).astype(jnp.bfloat16)
        middle = conv_apply(activated, conv_part[1])
        first_tap = conv_apply(activated, conv_part[0]).astype(jnp.bfloat16)
        last_tap = conv_apply(activated, conv_part[2]).astype(jnp.bfloat16)
        earlier, unused_later = reach(first_tap, spacing_gap)
        unused_earlier, later = reach(last_tap, spacing_gap)
        preact = (
            lax.optimization_barrier(earlier).astype(jnp.float32)
            + middle
            + lax.optimization_barrier(later).astype(jnp.float32)
        )
        hidden = jax.nn.gelu(preact).astype(jnp.bfloat16)
        stored.append((present_state, preact))
        branch = jnp.einsum("krh,hc->krc", hidden, proj_part, preferred_element_type=jnp.float32)
        present_state = (present_state.astype(jnp.float32) + branch).astype(jnp.bfloat16)
    return (present_state, stored)


def ring_gather(block):
    rows, width = block.shape
    span, lanes, cores = lax.axis_size("z"), lax.axis_size("xh"), lax.axis_size("core")
    here, core = lax.axis_index("z"), lax.axis_index("core")
    sign = 2 * core - 1
    route = []
    for z in range(span):
        for x in range(lanes):
            route.append(((z * lanes + x) * cores, (((z + 1) % span) * lanes + x) * cores))
            route.append(((z * lanes + x) * cores + 1, (((z - 1) % span) * lanes + x) * cores + 1))
    half = span // 2
    gathered = jnp.zeros((span, rows, width), block.dtype)
    gathered = lax.dynamic_update_slice(gathered, block[None], (here, 0, 0))
    current, received = block, []
    cut = rows // 2
    for step in range(1, half + 1):
        current = jnp.concatenate(
            [lax.ppermute(current[:cut], SEQ, route), lax.ppermute(current[cut:], SEQ, route)], axis=0
        )
        received.append(current)
        source = (here + sign * step) % span
        gathered = lax.dynamic_update_slice(gathered, current[None], (source, 0, 0))
    needed = span - half - 1
    early = needed // 2 + needed % 2
    for begin, end in ((0, early), (early, needed)):
        shared = lax.ppermute(jnp.stack(received[begin:end]), "core", [(0, 1), (1, 0)])
        for step in range(begin + 1, end + 1):
            source = (here - sign * step) % span
            gathered = lax.dynamic_update_slice(gathered, shared[step - 1 - begin][None], (source, 0, 0))
    return gathered


def ring_gather3(block):
    return ring_gather(block)


def gather_weights(conv_weight, proj_weight):
    conv, proj = conv_weight[0], proj_weight[0]
    taps, width = conv.shape[0] * conv.shape[1], conv.shape[3]
    both = jnp.concatenate([conv.reshape((taps,) + conv.shape[2:]), proj.reshape((-1,) + conv.shape[2:])], axis=0)
    both = lax.all_gather(lax.all_gather(both, "core", axis=0), "xh", axis=0)
    conv = both[:, :, :taps].reshape(both.shape[:2] + conv.shape)
    proj = both[:, :, taps:].reshape(both.shape[:2] + proj.shape)
    chip = conv.shape[0] * conv.shape[1]
    conv = jnp.moveaxis(conv.reshape((chip,) + conv.shape[2:]), 0, 2)
    conv = conv.reshape(taps * chip * conv.shape[3], width)
    proj = jnp.moveaxis(proj.reshape((chip,) + proj.shape[2:]), 0, 1)
    proj = proj.reshape(-1, width)
    conv_rows = conv.shape[0]
    gathered = ring_gather3(jnp.concatenate([conv, proj], axis=0))
    span = gathered.shape[0]
    conv = gathered[:, :conv_rows].reshape((span,) + conv_weight.shape[1:3] + (-1, width))
    conv = jnp.moveaxis(conv, 0, 2).reshape(conv_weight.shape[:3] + (-1, width))
    proj = gathered[:, conv_rows:].reshape((span, proj_weight.shape[1], -1, proj_weight.shape[3]))
    proj = jnp.moveaxis(proj, 0, 1).reshape(proj_weight.shape[:2] + (-1, proj_weight.shape[3]))
    return conv, proj


def local(fwd_input, bwd_input, bwd_cotangent, conv_weight, proj_weight):
    convolution_complete, proj_full = gather_weights(conv_weight, proj_weight)
    pieces = [
        (convolution_complete[0, depth_level], proj_full[0, depth_level])
        for depth_level in range(BLOCKS)
    ]
    both_out, both_stored = run_forward(jnp.concatenate([fwd_input, bwd_input], axis=0), pieces)
    forward_out = both_out[:1]
    stored = [(block_in[1:], preact[1:]) for block_in, preact in both_stored]
    cotangent = bwd_cotangent
    for depth_level in reversed(range(BLOCKS)):
        conv_part, proj_part = pieces[depth_level]
        spacing_gap = FIRST_DILATION * 4**depth_level
        block_in, preact = stored[depth_level]
        d_hidden = jnp.einsum(
            "krc,hc->krh", cotangent, proj_part, preferred_element_type=jnp.float32
        )
        d_preact = gelu_back(preact, d_hidden).astype(jnp.bfloat16)
        earlier, later = reach(d_preact, spacing_gap)
        d_act = (
            conv_transpose(later, conv_part[0])
            + conv_transpose(d_preact, conv_part[1])
            + conv_transpose(earlier, conv_part[2])
        )
        total = cotangent.astype(jnp.float32) + gelu_back(block_in.astype(jnp.float32), d_act)
        cotangent = total.astype(jnp.bfloat16)
    next_input = from_behind_2(forward_out, "section", 1)
    prev_cotangent = from_behind_2(cotangent, "section", -1)
    return (next_input, prev_cotangent)


def solution(mesh):
    seq, section = mesh.shape["seq"], mesh.shape["section"]
    split = Mesh(mesh.devices.reshape(seq // 4, 2, 2, section), SEQ + ("section",))
    in_specs = (
        P("section", SEQ, None),
        P("section", SEQ, None),
        P("section", SEQ, None),
        P("section", None, None, SEQ, None),
        P("section", None, SEQ, None),
    )
    out_specs = (P("section", SEQ, None), P("section", SEQ, None))
    return jax.shard_map(local, mesh=split, in_specs=in_specs, out_specs=out_specs, check_vma=False)
```

```python
import jax
import jax.numpy as jnp
from jax import lax
from jax.sharding import Mesh, PartitionSpec as P

BLOCKS = 2
FIRST_DILATION = 128
SEQ = ("z", "xh", "core")


def seq_size(axis):
    if isinstance(axis, tuple):
        size = 1
        for name in axis:
            size *= lax.axis_size(name)
        return size
    return lax.axis_size(axis)


def padded(x, sides, width):
    for axis, dim in sides:
        size, length = (seq_size(axis), x.shape[dim])
        up = [(i, (i + 1) % size) for i in range(size - 1)]
        down = [(j, i) for i, j in up]
        last = lax.slice_in_dim(x, length - width, length, axis=dim)
        initial = lax.slice_in_dim(x, 0, width, axis=dim)
        before = lax.ppermute(last, axis, up)
        after = lax.ppermute(initial, axis, down)
        x = jnp.concatenate([before, x, after], axis=dim)
    return x


def from_behind(block, axis, distance):
    devices = range(seq_size(axis))
    route = [(i - distance, i) for i in devices if i - distance in devices]
    return lax.ppermute(block, axis, route)


def from_behind_2(block, axis, distance):
    devices = range(seq_size(axis))
    route = [((i - distance) % len(devices), i) for i in devices]
    return lax.ppermute(block, axis, route)


def gelu_back(value, cotangent):
    return jax.vjp(jax.nn.gelu, value)[1](cotangent)[0]


def rounded(product):
    return lax.optimization_barrier(product.astype(jnp.bfloat16)).astype(jnp.float32)


def reach(values, spacing_gap):
    length = values.shape[1]
    if spacing_gap < length:
        padded_input = padded(values, ((SEQ, 1),), spacing_gap)
        return (padded_input[:, :length], padded_input[:, 2 * spacing_gap :])
    shard_hops = spacing_gap // length
    earlier = from_behind(values, SEQ, shard_hops)
    later = from_behind(values, SEQ, -shard_hops)
    return (earlier, later)


def conv_apply(values, weight):
    return jnp.einsum("krc,ch->krh", values, weight, preferred_element_type=jnp.float32)


def conv_transpose(values, weight):
    return jnp.einsum("krh,ch->krc", values, weight, preferred_element_type=jnp.float32)


def run_forward(present_state, pieces):
    stored = []
    for depth_level in range(BLOCKS):
        conv_part, proj_part = pieces[depth_level]
        spacing_gap = FIRST_DILATION * 4**depth_level
        activated = jax.nn.gelu(present_state.astype(jnp.float32)).astype(jnp.bfloat16)
        middle = conv_apply(activated, conv_part[1])
        first_tap = conv_apply(activated, conv_part[0]).astype(jnp.bfloat16)
        last_tap = conv_apply(activated, conv_part[2]).astype(jnp.bfloat16)
        earlier, unused_later = reach(first_tap, spacing_gap)
        unused_earlier, later = reach(last_tap, spacing_gap)
        preact = (
            lax.optimization_barrier(earlier).astype(jnp.float32)
            + middle
            + lax.optimization_barrier(later).astype(jnp.float32)
        )
        hidden = jax.nn.gelu(preact).astype(jnp.bfloat16)
        stored.append((present_state, preact))
        branch = jnp.einsum("krh,hc->krc", hidden, proj_part, preferred_element_type=jnp.float32)
        present_state = (present_state.astype(jnp.float32) + branch).astype(jnp.bfloat16)
    return (present_state, stored)


def ring_gather(block):
    rows, width = block.shape
    span, lanes, cores = lax.axis_size("z"), lax.axis_size("xh"), lax.axis_size("core")
    here, core = lax.axis_index("z"), lax.axis_index("core")
    sign = 2 * core - 1
    route = []
    for z in range(span):
        for x in range(lanes):
            route.append(((z * lanes + x) * cores, (((z + 1) % span) * lanes + x) * cores))
            route.append(((z * lanes + x) * cores + 1, (((z - 1) % span) * lanes + x) * cores + 1))
    half = span // 2
    gathered = jnp.zeros((span, rows, width), block.dtype)
    gathered = lax.dynamic_update_slice(gathered, block[None], (here, 0, 0))
    current, received = block, []
    cut = rows // 2
    for step in range(1, half + 1):
        third = rows // 3
        current = jnp.concatenate(
            [lax.ppermute(current[i * third : (i + 1) * third], SEQ, route) for i in range(3)], axis=0
        )
        received.append(current)
        source = (here + sign * step) % span
        gathered = lax.dynamic_update_slice(gathered, current[None], (source, 0, 0))
    needed = span - half - 1
    early = needed // 2 + needed % 2
    for begin, end in ((0, early), (early, needed)):
        shared = lax.ppermute(jnp.stack(received[begin:end]), "core", [(0, 1), (1, 0)])
        for step in range(begin + 1, end + 1):
            source = (here - sign * step) % span
            gathered = lax.dynamic_update_slice(gathered, shared[step - 1 - begin][None], (source, 0, 0))
    return gathered


def ring_gather3(block):
    return ring_gather(block)


def gather_weights(conv_weight, proj_weight):
    conv, proj = conv_weight[0], proj_weight[0]
    taps, width = conv.shape[0] * conv.shape[1], conv.shape[3]
    both = jnp.concatenate([conv.reshape((taps,) + conv.shape[2:]), proj.reshape((-1,) + conv.shape[2:])], axis=0)
    both = lax.all_gather(lax.all_gather(both, "core", axis=0), "xh", axis=0)
    conv = both[:, :, :taps].reshape(both.shape[:2] + conv.shape)
    proj = both[:, :, taps:].reshape(both.shape[:2] + proj.shape)
    chip = conv.shape[0] * conv.shape[1]
    conv = jnp.moveaxis(conv.reshape((chip,) + conv.shape[2:]), 0, 2)
    conv = conv.reshape(taps * chip * conv.shape[3], width)
    proj = jnp.moveaxis(proj.reshape((chip,) + proj.shape[2:]), 0, 1)
    proj = proj.reshape(-1, width)
    conv_rows = conv.shape[0]
    gathered = ring_gather3(jnp.concatenate([conv, proj], axis=0))
    span = gathered.shape[0]
    conv = gathered[:, :conv_rows].reshape((span,) + conv_weight.shape[1:3] + (-1, width))
    conv = jnp.moveaxis(conv, 0, 2).reshape(conv_weight.shape[:3] + (-1, width))
    proj = gathered[:, conv_rows:].reshape((span, proj_weight.shape[1], -1, proj_weight.shape[3]))
    proj = jnp.moveaxis(proj, 0, 1).reshape(proj_weight.shape[:2] + (-1, proj_weight.shape[3]))
    return conv, proj


def local(fwd_input, bwd_input, bwd_cotangent, conv_weight, proj_weight):
    convolution_complete, proj_full = gather_weights(conv_weight, proj_weight)
    pieces = [
        (convolution_complete[0, depth_level], proj_full[0, depth_level])
        for depth_level in range(BLOCKS)
    ]
    both_out, both_stored = run_forward(jnp.concatenate([fwd_input, bwd_input], axis=0), pieces)
    forward_out = both_out[:1]
    stored = [(block_in[1:], preact[1:]) for block_in, preact in both_stored]
    cotangent = bwd_cotangent
    for depth_level in reversed(range(BLOCKS)):
        conv_part, proj_part = pieces[depth_level]
        spacing_gap = FIRST_DILATION * 4**depth_level
        block_in, preact = stored[depth_level]
        d_hidden = jnp.einsum(
            "krc,hc->krh", cotangent, proj_part, preferred_element_type=jnp.float32
        )
        d_preact = gelu_back(preact, d_hidden).astype(jnp.bfloat16)
        earlier, later = reach(d_preact, spacing_gap)
        d_act = (
            conv_transpose(later, conv_part[0])
            + conv_transpose(d_preact, conv_part[1])
            + conv_transpose(earlier, conv_part[2])
        )
        total = cotangent.astype(jnp.float32) + gelu_back(block_in.astype(jnp.float32), d_act)
        cotangent = total.astype(jnp.bfloat16)
    next_input = from_behind_2(forward_out, "section", 1)
    prev_cotangent = from_behind_2(cotangent, "section", -1)
    return (next_input, prev_cotangent)


def solution(mesh):
    seq, section = mesh.shape["seq"], mesh.shape["section"]
    split = Mesh(mesh.devices.reshape(seq // 4, 2, 2, section), SEQ + ("section",))
    in_specs = (
        P("section", SEQ, None),
        P("section", SEQ, None),
        P("section", SEQ, None),
        P("section", None, None, SEQ, None),
        P("section", None, SEQ, None),
    )
    out_specs = (P("section", SEQ, None), P("section", SEQ, None))
    return jax.shard_map(local, mesh=split, in_specs=in_specs, out_specs=out_specs, check_vma=False)
```

```python
import jax
import jax.numpy as jnp
from jax import lax
from jax.sharding import Mesh, PartitionSpec as P

BLOCKS = 2
FIRST_DILATION = 128
SEQ = ("z", "xh", "core")


def seq_size(axis):
    if isinstance(axis, tuple):
        size = 1
        for name in axis:
            size *= lax.axis_size(name)
        return size
    return lax.axis_size(axis)


def padded(x, sides, width):
    for axis, dim in sides:
        size, length = (seq_size(axis), x.shape[dim])
        up = [(i, (i + 1) % size) for i in range(size - 1)]
        down = [(j, i) for i, j in up]
        last = lax.slice_in_dim(x, length - width, length, axis=dim)
        initial = lax.slice_in_dim(x, 0, width, axis=dim)
        before = lax.ppermute(last, axis, up)
        after = lax.ppermute(initial, axis, down)
        x = jnp.concatenate([before, x, after], axis=dim)
    return x


def from_behind(block, axis, distance):
    devices = range(seq_size(axis))
    route = [(i - distance, i) for i in devices if i - distance in devices]
    return lax.ppermute(block, axis, route)


def from_behind_2(block, axis, distance):
    devices = range(seq_size(axis))
    route = [((i - distance) % len(devices), i) for i in devices]
    return lax.ppermute(block, axis, route)


def gelu_back(value, cotangent):
    return jax.vjp(jax.nn.gelu, value)[1](cotangent)[0]


def rounded(product):
    return lax.optimization_barrier(product.astype(jnp.bfloat16)).astype(jnp.float32)


def reach(values, spacing_gap):
    length = values.shape[1]
    if spacing_gap < length:
        padded_input = padded(values, ((SEQ, 1),), spacing_gap)
        return (padded_input[:, :length], padded_input[:, 2 * spacing_gap :])
    shard_hops = spacing_gap // length
    earlier = from_behind(values, SEQ, shard_hops)
    later = from_behind(values, SEQ, -shard_hops)
    return (earlier, later)


def conv_apply(values, weight):
    return jnp.einsum("krc,ch->krh", values, weight, preferred_element_type=jnp.float32)


def conv_transpose(values, weight):
    return jnp.einsum("krh,ch->krc", values, weight, preferred_element_type=jnp.float32)


def run_forward(present_state, pieces):
    stored = []
    for depth_level in range(BLOCKS):
        conv_part, proj_part = pieces[depth_level]
        spacing_gap = FIRST_DILATION * 4**depth_level
        activated = jax.nn.gelu(present_state.astype(jnp.float32)).astype(jnp.bfloat16)
        middle = conv_apply(activated, conv_part[1])
        first_tap = conv_apply(activated, conv_part[0]).astype(jnp.bfloat16)
        last_tap = conv_apply(activated, conv_part[2]).astype(jnp.bfloat16)
        earlier, unused_later = reach(first_tap, spacing_gap)
        unused_earlier, later = reach(last_tap, spacing_gap)
        preact = (
            lax.optimization_barrier(earlier).astype(jnp.float32)
            + middle
            + lax.optimization_barrier(later).astype(jnp.float32)
        )
        hidden = jax.nn.gelu(preact).astype(jnp.bfloat16)
        stored.append((present_state, preact))
        branch = jnp.einsum("krh,hc->krc", hidden, proj_part, preferred_element_type=jnp.float32)
        present_state = (present_state.astype(jnp.float32) + branch).astype(jnp.bfloat16)
    return (present_state, stored)


def ring_gather(block):
    rows, width = block.shape
    span, lanes, cores = lax.axis_size("z"), lax.axis_size("xh"), lax.axis_size("core")
    here, core = lax.axis_index("z"), lax.axis_index("core")
    sign = 2 * core - 1
    route = []
    for z in range(span):
        for x in range(lanes):
            route.append(((z * lanes + x) * cores, (((z + 1) % span) * lanes + x) * cores))
            route.append(((z * lanes + x) * cores + 1, (((z - 1) % span) * lanes + x) * cores + 1))
    half = span // 2
    gathered = jnp.zeros((span, rows, width), block.dtype)
    gathered = lax.dynamic_update_slice(gathered, block[None], (here, 0, 0))
    current, received = block, []
    cut = rows // 2
    for step in range(1, half + 1):
        current = jnp.concatenate(
            [lax.ppermute(current[:cut], SEQ, route), lax.ppermute(current[cut:], SEQ, route)], axis=0
        )
        received.append(current)
        source = (here + sign * step) % span
        gathered = lax.dynamic_update_slice(gathered, current[None], (source, 0, 0))
    needed = span - half - 1
    early = needed - 2
    for begin, end in ((0, early), (early, needed)):
        shared = lax.ppermute(jnp.stack(received[begin:end]), "core", [(0, 1), (1, 0)])
        for step in range(begin + 1, end + 1):
            source = (here - sign * step) % span
            gathered = lax.dynamic_update_slice(gathered, shared[step - 1 - begin][None], (source, 0, 0))
    return gathered


def ring_gather3(block):
    return ring_gather(block)


def gather_weights(conv_weight, proj_weight):
    conv, proj = conv_weight[0], proj_weight[0]
    taps, width = conv.shape[0] * conv.shape[1], conv.shape[3]
    both = jnp.concatenate([conv.reshape((taps,) + conv.shape[2:]), proj.reshape((-1,) + conv.shape[2:])], axis=0)
    both = lax.all_gather(lax.all_gather(both, "core", axis=0), "xh", axis=0)
    conv = both[:, :, :taps].reshape(both.shape[:2] + conv.shape)
    proj = both[:, :, taps:].reshape(both.shape[:2] + proj.shape)
    chip = conv.shape[0] * conv.shape[1]
    conv = jnp.moveaxis(conv.reshape((chip,) + conv.shape[2:]), 0, 2)
    conv = conv.reshape(taps * chip * conv.shape[3], width)
    proj = jnp.moveaxis(proj.reshape((chip,) + proj.shape[2:]), 0, 1)
    proj = proj.reshape(-1, width)
    conv_rows = conv.shape[0]
    gathered = ring_gather3(jnp.concatenate([conv, proj], axis=0))
    span = gathered.shape[0]
    conv = gathered[:, :conv_rows].reshape((span,) + conv_weight.shape[1:3] + (-1, width))
    conv = jnp.moveaxis(conv, 0, 2).reshape(conv_weight.shape[:3] + (-1, width))
    proj = gathered[:, conv_rows:].reshape((span, proj_weight.shape[1], -1, proj_weight.shape[3]))
    proj = jnp.moveaxis(proj, 0, 1).reshape(proj_weight.shape[:2] + (-1, proj_weight.shape[3]))
    return conv, proj


def local(fwd_input, bwd_input, bwd_cotangent, conv_weight, proj_weight):
    convolution_complete, proj_full = gather_weights(conv_weight, proj_weight)
    pieces = [
        (convolution_complete[0, depth_level], proj_full[0, depth_level])
        for depth_level in range(BLOCKS)
    ]
    both_out, both_stored = run_forward(jnp.concatenate([fwd_input, bwd_input], axis=0), pieces)
    forward_out = both_out[:1]
    stored = [(block_in[1:], preact[1:]) for block_in, preact in both_stored]
    cotangent = bwd_cotangent
    for depth_level in reversed(range(BLOCKS)):
        conv_part, proj_part = pieces[depth_level]
        spacing_gap = FIRST_DILATION * 4**depth_level
        block_in, preact = stored[depth_level]
        d_hidden = jnp.einsum(
            "krc,hc->krh", cotangent, proj_part, preferred_element_type=jnp.float32
        )
        d_preact = gelu_back(preact, d_hidden).astype(jnp.bfloat16)
        earlier, later = reach(d_preact, spacing_gap)
        d_act = (
            conv_transpose(later, conv_part[0])
            + conv_transpose(d_preact, conv_part[1])
            + conv_transpose(earlier, conv_part[2])
        )
        total = cotangent.astype(jnp.float32) + gelu_back(block_in.astype(jnp.float32), d_act)
        cotangent = total.astype(jnp.bfloat16)
    next_input = from_behind_2(forward_out, "section", 1)
    prev_cotangent = from_behind_2(cotangent, "section", -1)
    return (next_input, prev_cotangent)


def solution(mesh):
    seq, section = mesh.shape["seq"], mesh.shape["section"]
    split = Mesh(mesh.devices.reshape(seq // 4, 2, 2, section), SEQ + ("section",))
    in_specs = (
        P("section", SEQ, None),
        P("section", SEQ, None),
        P("section", SEQ, None),
        P("section", None, None, SEQ, None),
        P("section", None, SEQ, None),
    )
    out_specs = (P("section", SEQ, None), P("section", SEQ, None))
    return jax.shard_map(local, mesh=split, in_specs=in_specs, out_specs=out_specs, check_vma=False)
```
